32 devices in a mesh: groups: 2 (over y), rows: 4 (over z), cols: 4 (over x, core).
Axes of the slice: x: 2, y: 2, z: 4, core: 2. Of those that a mesh axis runs over, the one named last changes fastest.
Arguments:
- points: bfloat16 [6144, 128], P(('groups', 'rows', 'cols')), parts along dimension 0, as said below
- solution: float32 [6144, 128], P(('groups', 'rows', 'cols')), parts along dimension 0, may hold values from -6 to 6
- targets: float32 [6144, 128], P(('groups', 'rows', 'cols')), parts along dimension 0, may hold values from -40 to 40, as said below
- inducing: int32 [2048], P('groups'), parts along dimension 0, may hold values from 0 to 3071, as said below
- woodbury_inverse: float32 [2048, 1024], P('groups'), parts along dimension 0, may hold values from -1 to 7, as said below
Outputs:
- new_solution: float32 [6144, 128], P(('groups', 'rows', 'cols')), parts along dimension 0
- residual: float32 [6144, 128], P(('groups', 'rows', 'cols')), parts along dimension 0
- relative_norm: float32 [256], P('groups'), parts along dimension 0
The draws below stay inside these ranges and needn't reach their ends.
There are 2 independent parts, one for each index of `groups`. The reference program is written for one: setup_inputs(seed, part) draws one part's arguments, and reference() takes and returns one part's arrays. A program takes and returns all parts, laid end to end along the dimension named above; each array names one. Nothing has to cross between parts.
Inputs may be any that keep to these rules, and one draw needn't show every extreme that they name: `points`: input locations. targets of each right-hand side have their own scale. `inducing`: indices into this problem's points. `woodbury_inverse`: symmetric.
All inputs are finite; a program needn't handle non-finite values.
Results may differ from the reference program's by a relative error of at most 0.0031.
Values may be sent and summed in bfloat16 or wider, within the bound.
No kernel may reach another device: no remote copies, remote signals or barrier semaphores. Data moves between devices by JAX's collectives and lax.ppermute only.
A program may use at most 64 MiB of HBM per device.

```python
import math
import jax
import jax.numpy as jnp
from jax import lax

F = 128
R = 128
M = 1024
NDEV = 192
POINTS = 3072
N_ROWS = 4
N_COLS = 4


def draw_points(key, part):
    first, second, third = jax.random.split(key, 3)
    gamma = 2.5 / F
    order = jax.random.permutation(second, F)
    strong = order < 4
    level = jax.random.uniform(third, (F,), jnp.float32, 0.0, 1.0)
    strong_q = jnp.exp(math.log(0.35) + level * math.log(2.0))
    weak_q = jnp.exp(math.log(0.005) + level * math.log(3.0))
    scale = jnp.sqrt(jnp.where(strong, strong_q, weak_q) / gamma)
    base = jnp.clip(jax.random.normal(first, (POINTS, F), jnp.float32), -4.0, 4.0)
    return (base * scale[None, :]).astype(jnp.bfloat16)


def draw_targets(key, part):
    first, second = jax.random.split(key)
    position = jnp.arange(POINTS, dtype=jnp.float32)
    rise = 1.0 + 2.0 * position / POINTS
    column_scale = jnp.exp(jax.random.uniform(second, (R,), jnp.float32, math.log(0.25), math.log(2.5)))
    base = jnp.clip(jax.random.normal(first, (POINTS, R), jnp.float32), -4.0, 4.0)
    return base * rise[:, None] * column_scale[None, :]


def draw_inducing(key, part):
    picked = jax.random.randint(key, (M,), 0, POINTS, dtype=jnp.int32)
    return picked.at[0].set(0).at[M - 1].set(POINTS - 1)


def draw_woodbury_inverse(key, part):
    first, second = jax.random.split(key)
    diagonal = jnp.exp(jax.random.uniform(first, (M,), jnp.float32, math.log(2.5), math.log(6.0)))
    noise = jnp.clip(jax.random.normal(second, (M, M), jnp.float32), -4.0, 4.0)
    symmetric = (noise + noise.T) * (0.7071 / math.sqrt(M))
    return symmetric + jnp.diag(diagonal)


def shard_levels(key, dims, cuts, least, largest):
    def one(axis_at, parts):
        draws = jax.random.uniform(jax.random.fold_in(jax.random.fold_in(key, 6), axis_at), (parts,), jnp.float32, least / len(cuts), largest / len(cuts))
        return jnp.repeat(jnp.exp(draws), dims[axis_at] // parts).reshape((-1,) + (1,) * (len(dims) - axis_at - 1))

    gain = one(*cuts[0])
    for cut in cuts[1:]:
        gain = gain * one(*cut)
    return gain


def normal_values(own_key, shape, deviation, most, shards=(), held_as=jnp.bfloat16):
    values = jax.random.normal(own_key, shape, jnp.float32) * deviation
    if len(shards) > 0:
        values = shard_levels(own_key, shape, shards, -0.22, 0.18) * values
    return jnp.clip(values, min=-most, max=most).astype(held_as)


def setup_inputs(seed: int = 0, part: int = 0) -> dict:
    arg_keys = jax.random.split(jax.random.key(seed), 6)
    part_splits = jax.random.split(jax.random.fold_in(arg_keys[5], part), 6)
    return {
        "points": draw_points(jax.random.fold_in(jax.random.fold_in(arg_keys[5], part), 71), part),
        "solution": normal_values(part_splits[1], (POINTS, R), 1.0, 6.0, ((0, 16),), jnp.float32),
        "targets": draw_targets(jax.random.fold_in(jax.random.fold_in(arg_keys[5], part), 71), part),
        "inducing": draw_inducing(jax.random.fold_in(jax.random.fold_in(arg_keys[5], part), 71), part),
        "woodbury_inverse": draw_woodbury_inverse(jax.random.fold_in(jax.random.fold_in(arg_keys[5], part), 71), part),
    }


noise_level = 0.5

def reference(points, solution, targets, inducing, woodbury_inverse):
    gamma = 2.5 / F
    sq = lax.optimization_barrier(jnp.sum(jnp.square(points.astype(jnp.float32)), axis=1))
    solution_b = solution.astype(jnp.bfloat16)
    block = NDEV * N_COLS

    def one_block(index):
        start = (index * block).astype(jnp.int32)
        rows_x = lax.dynamic_slice_in_dim(points, start, block, 0)
        rows_sq = lax.dynamic_slice_in_dim(sq, start, block, 0)
        inner = jnp.dot(rows_x, points.T, preferred_element_type=jnp.float32)
        kernel = jnp.exp(-gamma * (rows_sq[:, None] + sq[None, :] - 2.0 * inner)).astype(jnp.bfloat16)
        return jnp.dot(kernel, solution_b, preferred_element_type=jnp.float32)
    kernel_product = lax.map(one_block, jnp.arange(N_ROWS, dtype=jnp.int32)).reshape(POINTS, R)
    residual = targets - kernel_product - noise_level * solution
    centers = points[inducing.astype(jnp.int32)]
    sqc = lax.optimization_barrier(jnp.sum(jnp.square(centers.astype(jnp.float32)), axis=1))
    inner_c = jnp.dot(points, centers.T, preferred_element_type=jnp.float32)
    cross = jnp.exp(-gamma * (sq[:, None] + sqc[None, :] - 2.0 * inner_c)).astype(jnp.bfloat16)
    residual_b = residual.astype(jnp.bfloat16)
    projected = jnp.dot(cross.T, residual_b, preferred_element_type=jnp.float32)
    weights = jnp.dot(woodbury_inverse, projected, precision=lax.Precision.HIGHEST)
    correction = jnp.dot(cross, weights.astype(jnp.bfloat16), preferred_element_type=jnp.float32)
    new_solution = solution + (residual - correction) / noise_level
    res_sq = lax.optimization_barrier(jnp.sum(residual * residual, axis=0))
    tar_sq = lax.optimization_barrier(jnp.sum(targets * targets, axis=0))
    relative_norm = jnp.sqrt(res_sq / (tar_sq + 1e-06))
    return (new_solution, residual, relative_norm)
```

```python
import jax
import jax.numpy as jnp
from jax import lax
from jax.sharding import PartitionSpec as P

F = 128

noise_level = 0.5

COLUMN_CHUNK = 3072


def square_norms(values):
    return jnp.sum(jnp.square(values.astype(jnp.float32)), axis=1)


def rbf_tile(left_x, left_sq, right_x, right_sq, gamma):
    inner = lax.dot_general(
        left_x, right_x, (((1,), (1,)), ((), ())), preferred_element_type=jnp.float32
    )
    return jnp.exp(-gamma * (left_sq[:, None] + right_sq[None, :] - 2.0 * inner)).astype(
        jnp.bfloat16
    )


def kernel_product(own_x, own_sq, all_x, all_sq, all_v, gamma):
    total = all_x.shape[0]
    chunk = min(COLUMN_CHUNK, total)
    if total % chunk != 0:
        chunk = total
    steps = total // chunk

    def piece(start):
        x = lax.dynamic_slice_in_dim(all_x, start, chunk, 0)
        s = lax.dynamic_slice_in_dim(all_sq, start, chunk, 0)
        v = lax.dynamic_slice_in_dim(all_v, start, chunk, 0)
        k = rbf_tile(own_x, own_sq, x, s, gamma)
        return jnp.dot(k, v, preferred_element_type=jnp.float32)

    if steps == 1:
        return piece(0)

    def body(i, acc):
        return acc + piece(i * chunk)

    init = jnp.zeros((own_x.shape[0], all_v.shape[1]), jnp.float32)
    return lax.fori_loop(0, steps, body, init)


def local(points, solution, targets, inducing, woodbury_inverse):
    gamma = 2.5 / F
    solution_b = solution.astype(jnp.bfloat16)
    packed = jnp.concatenate([points, solution_b], axis=1)
    gathered = lax.all_gather(packed, ("rows", "cols"), axis=0, tiled=True)
    all_x = gathered[:, :F]
    all_v = gathered[:, F:]
    all_sq = square_norms(all_x)
    own_sq = square_norms(points)
    kp = kernel_product(points, own_sq, all_x, all_sq, all_v, gamma)
    residual = targets - kp - noise_level * solution
    centers = jnp.take(all_x, inducing, axis=0)
    cross = rbf_tile(points, own_sq, centers, square_norms(centers), gamma)
    residual_b = residual.astype(jnp.bfloat16)
    projected_local = lax.dot_general(
        cross, residual_b, (((0,), (0,)), ((), ())), preferred_element_type=jnp.float32
    )
    res_local = jnp.sum(residual * residual, axis=0)
    tar_local = jnp.sum(targets * targets, axis=0)
    stacked = jnp.concatenate([projected_local, res_local[None], tar_local[None]], axis=0)
    summed = lax.psum(stacked, ("rows", "cols"))
    m = projected_local.shape[0]
    projected = summed[:m]
    res_sq = summed[m]
    tar_sq = summed[m + 1]
    weights = jnp.dot(woodbury_inverse, projected, precision=lax.Precision.HIGHEST)
    correction = jnp.dot(cross, weights.astype(jnp.bfloat16), preferred_element_type=jnp.float32)
    new_solution = solution + (residual - correction) / noise_level
    relative_norm = jnp.sqrt(res_sq / (tar_sq + 1e-06))
    return (new_solution, residual, relative_norm)


def solution(mesh):
    return jax.shard_map(
        local,
        mesh=mesh,
        in_specs=(
            P(("groups", "rows", "cols"), None),
            P(("groups", "rows", "cols"), None),
            P(("groups", "rows", "cols"), None),
            P("groups"),
            P("groups", None),
        ),
        out_specs=(
            P(("groups", "rows", "cols"), None),
            P(("groups", "rows", "cols"), None),
            P("groups"),
        ),
        check_vma=False,
    )
```

```python
import jax
import jax.numpy as jnp
from jax import lax
from jax.sharding import PartitionSpec as P

F = 128

noise_level = 0.5

COLUMN_CHUNK = 3072


def square_norms(values):
    return jnp.sum(jnp.square(values.astype(jnp.float32)), axis=1)


def rbf_tile(left_x, left_sq, right_x, right_sq, gamma):
    inner = lax.dot_general(
        left_x, right_x, (((1,), (1,)), ((), ())), preferred_element_type=jnp.float32
    )
    return jnp.exp(-gamma * (left_sq[:, None] + right_sq[None, :] - 2.0 * inner)).astype(
        jnp.bfloat16
    )


def kernel_product(own_x, own_sq, all_x, all_sq, all_v, gamma):
    total = all_x.shape[0]
    chunk = min(COLUMN_CHUNK, total)
    if total % chunk != 0:
        chunk = total
    steps = total // chunk

    def piece(start):
        x = lax.dynamic_slice_in_dim(all_x, start, chunk, 0)
        s = lax.dynamic_slice_in_dim(all_sq, start, chunk, 0)
        v = lax.dynamic_slice_in_dim(all_v, start, chunk, 0)
        k = rbf_tile(own_x, own_sq, x, s, gamma)
        return jnp.dot(k, v, preferred_element_type=jnp.float32)

    if steps == 1:
        return piece(0)

    def body(i, acc):
        return acc + piece(i * chunk)

    init = jnp.zeros((own_x.shape[0], all_v.shape[1]), jnp.float32)
    return lax.fori_loop(0, steps, body, init)


def split_bf16(values):
    hi = values.astype(jnp.bfloat16)
    lo = (values - hi.astype(jnp.float32)).astype(jnp.bfloat16)
    return hi, lo


def projected_all(all_x, all_sq, centers, centers_sq, residual_b_all, gamma):
    total = all_x.shape[0]
    chunk = min(COLUMN_CHUNK, total)
    if total % chunk != 0:
        chunk = total
    steps = total // chunk

    def piece(start):
        x = lax.dynamic_slice_in_dim(all_x, start, chunk, 0)
        s = lax.dynamic_slice_in_dim(all_sq, start, chunk, 0)
        r = lax.dynamic_slice_in_dim(residual_b_all, start, chunk, 0)
        c = rbf_tile(x, s, centers, centers_sq, gamma)
        return lax.dot_general(c, r, (((0,), (0,)), ((), ())), preferred_element_type=jnp.float32)

    if steps == 1:
        return piece(0)

    def body(i, acc):
        return acc + piece(i * chunk)

    init = jnp.zeros((centers.shape[0], residual_b_all.shape[1]), jnp.float32)
    return lax.fori_loop(0, steps, body, init)


def local(points, solution, targets, inducing, woodbury_inverse):
    gamma = 2.5 / F
    n_local = points.shape[0]
    solution_b = solution.astype(jnp.bfloat16)
    packed = jnp.concatenate([points, solution_b], axis=1)
    gathered = lax.all_gather(packed, ("rows", "cols"), axis=0, tiled=True)
    all_x = gathered[:, :F]
    all_v = gathered[:, F:]
    all_sq = square_norms(all_x)
    own_sq = square_norms(points)
    kp = kernel_product(points, own_sq, all_x, all_sq, all_v, gamma)
    residual = targets - kp - noise_level * solution
    centers = jnp.take(all_x, inducing, axis=0)
    centers_sq = square_norms(centers)
    cross = rbf_tile(points, own_sq, centers, centers_sq, gamma)
    residual_b = residual.astype(jnp.bfloat16)
    res_local = jnp.sum(residual * residual, axis=0)
    tar_local = jnp.sum(targets * targets, axis=0)
    hi, lo = split_bf16(jnp.stack([res_local, tar_local]))
    pad = jnp.zeros((12, residual_b.shape[1]), jnp.bfloat16)
    sent = jnp.concatenate([residual_b, hi, lo, pad], axis=0)
    rows_sent = sent.shape[0]
    got = lax.all_gather(sent, ("rows", "cols"), axis=0, tiled=False)
    residual_b_all = got[:, :n_local].reshape(-1, residual_b.shape[1])
    norm_parts = got[:, n_local:n_local + 2].astype(jnp.float32) + got[:, n_local + 2:n_local + 4].astype(
        jnp.float32
    )
    norms = jnp.sum(norm_parts, axis=0)
    res_sq = norms[0]
    tar_sq = norms[1]
    projected = projected_all(all_x, all_sq, centers, centers_sq, residual_b_all, gamma)
    weights = jnp.dot(woodbury_inverse, projected, precision=lax.Precision.HIGHEST)
    correction = jnp.dot(cross, weights.astype(jnp.bfloat16), preferred_element_type=jnp.float32)
    new_solution = solution + (residual - correction) / noise_level
    relative_norm = jnp.sqrt(res_sq / (tar_sq + 1e-06))
    return (new_solution, residual, relative_norm)


def solution(mesh):
    return jax.shard_map(
        local,
        mesh=mesh,
        in_specs=(
            P(("groups", "rows", "cols"), None),
            P(("groups", "rows", "cols"), None),
            P(("groups", "rows", "cols"), None),
            P("groups"),
            P("groups", None),
        ),
        out_specs=(
            P(("groups", "rows", "cols"), None),
            P(("groups", "rows", "cols"), None),
            P("groups"),
        ),
        check_vma=False,
    )
```

```python
import jax
import jax.numpy as jnp
from jax import lax
from jax.sharding import PartitionSpec as P

F = 128


noise_level = 0.5

COLUMN_CHUNK = 3072


def square_norms(values):
    return jnp.sum(jnp.square(values.astype(jnp.float32)), axis=1)


def rbf_tile(left_x, left_sq, right_x, right_sq, gamma):
    inner = lax.dot_general(
        left_x, right_x, (((1,), (1,)), ((), ())), preferred_element_type=jnp.float32
    )
    return jnp.exp(-gamma * (left_sq[:, None] + right_sq[None, :] - 2.0 * inner)).astype(
        jnp.bfloat16
    )


def kernel_product(own_x, own_sq, all_x, all_sq, all_v, gamma):
    total = all_x.shape[0]
    chunk = min(COLUMN_CHUNK, total)
    if total % chunk != 0:
        chunk = total
    steps = total // chunk

    def piece(start):
        x = lax.dynamic_slice_in_dim(all_x, start, chunk, 0)
        s = lax.dynamic_slice_in_dim(all_sq, start, chunk, 0)
        v = lax.dynamic_slice_in_dim(all_v, start, chunk, 0)
        k = rbf_tile(own_x, own_sq, x, s, gamma)
        return jnp.dot(k, v, preferred_element_type=jnp.float32)

    if steps == 1:
        return piece(0)

    def body(i, acc):
        return acc + piece(i * chunk)

    init = jnp.zeros((own_x.shape[0], all_v.shape[1]), jnp.float32)
    return lax.fori_loop(0, steps, body, init)


def split_bf16(values):
    hi = lax.reduce_precision(values, exponent_bits=8, mantissa_bits=7)
    lo = values - hi
    return hi.astype(jnp.bfloat16), lo.astype(jnp.bfloat16)


PERMUTE_GROUP_MAX = 16


def group_index():
    return lax.axis_index("rows") * lax.axis_size("cols") + lax.axis_index("cols")


def gather_blocks(block):
    n = lax.axis_size("rows") * lax.axis_size("cols")
    if n > PERMUTE_GROUP_MAX:
        got = lax.all_gather(block, ("rows", "cols"), axis=0, tiled=False)
        me = group_index()
        order = (me - jnp.arange(n, dtype=jnp.int32)) % n
        return jnp.take(got, order, axis=0)
    moved = [block]
    for k in range(1, n):
        perm = [(i, (i + k) % n) for i in range(n)]
        moved.append(lax.ppermute(block, ("rows", "cols"), perm))
    return jnp.stack(moved)


def projected_all(all_x, all_sq, centers, centers_sq, residual_b_all, gamma):
    total = all_x.shape[0]
    chunk = min(COLUMN_CHUNK, total)
    if total % chunk != 0:
        chunk = total
    steps = total // chunk

    def piece(start):
        x = lax.dynamic_slice_in_dim(all_x, start, chunk, 0)
        s = lax.dynamic_slice_in_dim(all_sq, start, chunk, 0)
        r = lax.dynamic_slice_in_dim(residual_b_all, start, chunk, 0)
        c = rbf_tile(x, s, centers, centers_sq, gamma)
        return lax.dot_general(c, r, (((0,), (0,)), ((), ())), preferred_element_type=jnp.float32)

    if steps == 1:
        return piece(0)

    def body(i, acc):
        return acc + piece(i * chunk)

    init = jnp.zeros((centers.shape[0], residual_b_all.shape[1]), jnp.float32)
    return lax.fori_loop(0, steps, body, init)


def local(points, solution, targets, inducing, woodbury_inverse):
    gamma = 2.5 / F
    n_local = points.shape[0]
    n = lax.axis_size("rows") * lax.axis_size("cols")
    me = group_index()
    solution_b = solution.astype(jnp.bfloat16)
    packed = jnp.concatenate([points, solution_b], axis=1)
    gathered = gather_blocks(packed).reshape(n * n_local, 2 * F)
    all_x = gathered[:, :F]
    all_v = gathered[:, F:]
    all_sq = square_norms(all_x)
    own_sq = square_norms(points)
    kp = kernel_product(points, own_sq, all_x, all_sq, all_v, gamma)
    residual = targets - kp - noise_level * solution
    owner = inducing // n_local
    position = ((me - owner) % n) * n_local + inducing % n_local
    centers = jnp.take(all_x, position, axis=0)
    centers_sq = square_norms(centers)
    cross = rbf_tile(points, own_sq, centers, centers_sq, gamma)
    residual_b = residual.astype(jnp.bfloat16)
    res_local = jnp.sum(residual * residual, axis=0)
    tar_local = jnp.sum(targets * targets, axis=0)
    hi, lo = split_bf16(jnp.stack([res_local, tar_local]))
    pad = jnp.zeros((12, residual_b.shape[1]), jnp.bfloat16)
    sent = jnp.concatenate([residual_b, hi, lo, pad], axis=0)
    got = gather_blocks(sent)
    residual_b_all = got[:, :n_local].reshape(-1, residual_b.shape[1])
    norm_parts = got[:, n_local:n_local + 2].astype(jnp.float32) + got[:, n_local + 2:n_local + 4].astype(
        jnp.float32
    )
    norms = jnp.sum(norm_parts, axis=0)
    res_sq = norms[0]
    tar_sq = norms[1]
    projected = projected_all(all_x, all_sq, centers, centers_sq, residual_b_all, gamma)
    weights = jnp.dot(woodbury_inverse, projected, precision=lax.Precision.HIGH)
    correction = jnp.dot(cross, weights.astype(jnp.bfloat16), preferred_element_type=jnp.float32)
    new_solution = solution + (residual - correction) / noise_level
    relative_norm = jnp.sqrt(res_sq / (tar_sq + 1e-06))
    return (new_solution, residual, relative_norm)


def solution(mesh):
    return jax.shard_map(
        local,
        mesh=mesh,
        in_specs=(
            P(("groups", "rows", "cols"), None),
            P(("groups", "rows", "cols"), None),
            P(("groups", "rows", "cols"), None),
            P("groups"),
            P("groups", None),
        ),
        out_specs=(
            P(("groups", "rows", "cols"), None),
            P(("groups", "rows", "cols"), None),
            P("groups"),
        ),
        check_vma=False,
    )
```

```python
import jax
import jax.numpy as jnp
from jax import lax
from jax.sharding import PartitionSpec as P

F = 128


noise_level = 0.5

COLUMN_CHUNK = 3072


def square_norms(values):
    return jnp.sum(jnp.square(values.astype(jnp.float32)), axis=1)


def rbf_tile(left_x, left_sq, right_x, right_sq, gamma):
    inner = lax.dot_general(
        left_x, right_x, (((1,), (1,)), ((), ())), preferred_element_type=jnp.float32
    )
    return jnp.exp(-gamma * (left_sq[:, None] + right_sq[None, :] - 2.0 * inner)).astype(
        jnp.bfloat16
    )


def kernel_product(own_x, own_sq, all_x, all_sq, all_v, gamma):
    total = all_x.shape[0]
    chunk = min(COLUMN_CHUNK, total)
    if total % chunk != 0:
        chunk = total
    steps = total // chunk

    def piece(start):
        x = lax.dynamic_slice_in_dim(all_x, start, chunk, 0)
        s = lax.dynamic_slice_in_dim(all_sq, start, chunk, 0)
        v = lax.dynamic_slice_in_dim(all_v, start, chunk, 0)
        k = rbf_tile(own_x, own_sq, x, s, gamma)
        return jnp.dot(k, v, preferred_element_type=jnp.float32)

    if steps == 1:
        return piece(0)

    def body(i, acc):
        return acc + piece(i * chunk)

    init = jnp.zeros((own_x.shape[0], all_v.shape[1]), jnp.float32)
    return lax.fori_loop(0, steps, body, init)


def split_bf16(values):
    hi = lax.reduce_precision(values, exponent_bits=8, mantissa_bits=7)
    lo = values - hi
    return hi.astype(jnp.bfloat16), lo.astype(jnp.bfloat16)


PERMUTE_GROUP_MAX = 16


def group_index():
    return lax.axis_index("rows") * lax.axis_size("cols") + lax.axis_index("cols")


def is_power_of_two(n):
    return n & (n - 1) == 0


def axis_gather(value, axis):
    n = lax.axis_size(axis)
    if not is_power_of_two(n):
        moved = [value]
        for k in range(1, n):
            perm = [(i, (i + k) % n) for i in range(n)]
            moved.append(lax.ppermute(value, axis, perm))
        return jnp.concatenate(moved, axis=0)
    held = value
    bit = n // 2
    while bit >= 1:
        perm = [(i, i ^ bit) for i in range(n)]
        held = jnp.concatenate([held, lax.ppermute(held, axis, perm)], axis=0)
        bit //= 2
    return held


def axis_piece(axis, owner):
    n = lax.axis_size(axis)
    me = lax.axis_index(axis)
    if not is_power_of_two(n):
        return (me - owner) % n
    d = me ^ owner
    steps = n.bit_length() - 1
    piece = jnp.zeros_like(d)
    for j in range(steps):
        piece = piece + (((d >> (steps - 1 - j)) & 1) << j)
    return piece


def gather_blocks(block):
    n = lax.axis_size("rows") * lax.axis_size("cols")
    if n > PERMUTE_GROUP_MAX:
        got = lax.all_gather(block, ("rows", "cols"), axis=0, tiled=False)
        order = relative_order(jnp.arange(n, dtype=jnp.int32))
        return jnp.take(got, jnp.argsort(order), axis=0).reshape(-1, block.shape[1])
    return axis_gather(axis_gather(block, "rows"), "cols")


def relative_order(owner):
    n_rows = lax.axis_size("rows")
    n_cols = lax.axis_size("cols")
    return axis_piece("cols", owner % n_cols) * n_rows + axis_piece("rows", owner // n_cols)


def projected_all(all_x, all_sq, centers, centers_sq, residual_b_all, gamma):
    total = all_x.shape[0]
    chunk = min(COLUMN_CHUNK, total)
    if total % chunk != 0:
        chunk = total
    steps = total // chunk

    def piece(start):
        x = lax.dynamic_slice_in_dim(all_x, start, chunk, 0)
        s = lax.dynamic_slice_in_dim(all_sq, start, chunk, 0)
        r = lax.dynamic_slice_in_dim(residual_b_all, start, chunk, 0)
        c = rbf_tile(x, s, centers, centers_sq, gamma)
        return lax.dot_general(c, r, (((0,), (0,)), ((), ())), preferred_element_type=jnp.float32)

    if steps == 1:
        return piece(0)

    def body(i, acc):
        return acc + piece(i * chunk)

    init = jnp.zeros((centers.shape[0], residual_b_all.shape[1]), jnp.float32)
    return lax.fori_loop(0, steps, body, init)


def local(points, solution, targets, inducing, woodbury_inverse):
    gamma = 2.5 / F
    n_local = points.shape[0]
    n = lax.axis_size("rows") * lax.axis_size("cols")
    me = group_index()
    solution_b = solution.astype(jnp.bfloat16)
    packed = jnp.concatenate([points, solution_b], axis=1)
    gathered = gather_blocks(packed)
    all_x = gathered[:, :F]
    all_v = gathered[:, F:]
    all_sq = square_norms(all_x)
    own_sq = square_norms(points)
    kp = kernel_product(points, own_sq, all_x, all_sq, all_v, gamma)
    residual = targets - kp - noise_level * solution
    owner = inducing // n_local
    position = relative_order(owner) * n_local + inducing % n_local
    centers = jnp.take(all_x, position, axis=0)
    centers_sq = square_norms(centers)
    cross = rbf_tile(points, own_sq, centers, centers_sq, gamma)
    residual_b = residual.astype(jnp.bfloat16)
    res_local = jnp.sum(residual * residual, axis=0)
    tar_local = jnp.sum(targets * targets, axis=0)
    hi, lo = split_bf16(jnp.stack([res_local, tar_local]))
    extra = jnp.zeros((16, residual_b.shape[1]), jnp.bfloat16).at[0:2].set(hi).at[2:4].set(lo)
    sent = jnp.concatenate([residual_b, extra], axis=0)
    got = gather_blocks(sent).reshape(n, sent.shape[0], sent.shape[1])
    residual_b_all = got[:, :n_local].reshape(-1, residual_b.shape[1])
    norm_parts = got[:, n_local:n_local + 2].astype(jnp.float32) + got[:, n_local + 2:n_local + 4].astype(
        jnp.float32
    )
    norms = jnp.sum(norm_parts, axis=0)
    res_sq = norms[0]
    tar_sq = norms[1]
    projected = projected_all(all_x, all_sq, centers, centers_sq, residual_b_all, gamma)
    weights = jnp.dot(woodbury_inverse, projected, precision=lax.Precision.HIGH)
    correction = jnp.dot(cross, weights.astype(jnp.bfloat16), preferred_element_type=jnp.float32)
    new_solution = solution + (residual - correction) / noise_level
    relative_norm = jnp.sqrt(res_sq / (tar_sq + 1e-06))
    return (new_solution, residual, relative_norm)


def solution(mesh):
    return jax.shard_map(
        local,
        mesh=mesh,
        in_specs=(
            P(("groups", "rows", "cols"), None),
            P(("groups", "rows", "cols"), None),
            P(("groups", "rows", "cols"), None),
            P("groups"),
            P("groups", None),
        ),
        out_specs=(
            P(("groups", "rows", "cols"), None),
            P(("groups", "rows", "cols"), None),
            P("groups"),
        ),
        check_vma=False,
    )
```

```python
import jax
import jax.numpy as jnp
from jax import lax
from jax.sharding import PartitionSpec as P

F = 128


noise_level = 0.5

COLUMN_CHUNK = 3072


def square_norms(values):
    return jnp.sum(jnp.square(values.astype(jnp.float32)), axis=1)


def rbf_tile(left_x, left_sq, right_x, right_sq, gamma):
    inner = lax.dot_general(
        left_x, right_x, (((1,), (1,)), ((), ())), preferred_element_type=jnp.float32
    )
    return jnp.exp(-gamma * (left_sq[:, None] + right_sq[None, :] - 2.0 * inner)).astype(
        jnp.bfloat16
    )


def kernel_product(own_x, own_sq, all_x, all_sq, all_v, gamma):
    total = all_x.shape[0]
    chunk = min(COLUMN_CHUNK, total)
    if total % chunk != 0:
        chunk = total
    steps = total // chunk

    def piece(start):
        x = lax.dynamic_slice_in_dim(all_x, start, chunk, 0)
        s = lax.dynamic_slice_in_dim(all_sq, start, chunk, 0)
        v = lax.dynamic_slice_in_dim(all_v, start, chunk, 0)
        k = rbf_tile(own_x, own_sq, x, s, gamma)
        return jnp.dot(k, v, preferred_element_type=jnp.float32)

    if steps == 1:
        return piece(0)

    def body(i, acc):
        return acc + piece(i * chunk)

    init = jnp.zeros((own_x.shape[0], all_v.shape[1]), jnp.float32)
    return lax.fori_loop(0, steps, body, init)


def split_bf16(values):
    hi = lax.reduce_precision(values, exponent_bits=8, mantissa_bits=7)
    lo = values - hi
    return hi.astype(jnp.bfloat16), lo.astype(jnp.bfloat16)


PERMUTE_GROUP_MAX = 16


def group_index():
    return lax.axis_index("rows") * lax.axis_size("cols") + lax.axis_index("cols")


def is_power_of_two(n):
    return n & (n - 1) == 0


RING_AXES = ("rows",)


def uses_ring(axis):
    return axis in RING_AXES or not is_power_of_two(lax.axis_size(axis))


def axis_gather(value, axis):
    n = lax.axis_size(axis)
    if uses_ring(axis):
        moved = [value]
        for k in range(1, n):
            perm = [(i, (i + k) % n) for i in range(n)]
            moved.append(lax.ppermute(value, axis, perm))
        return jnp.concatenate(moved, axis=0)
    held = value
    bit = n // 2
    while bit >= 1:
        perm = [(i, i ^ bit) for i in range(n)]
        held = jnp.concatenate([held, lax.ppermute(held, axis, perm)], axis=0)
        bit //= 2
    return held


def axis_piece(axis, owner):
    n = lax.axis_size(axis)
    me = lax.axis_index(axis)
    if uses_ring(axis):
        return (me - owner) % n
    d = me ^ owner
    steps = n.bit_length() - 1
    piece = jnp.zeros_like(d)
    for j in range(steps):
        piece = piece + (((d >> (steps - 1 - j)) & 1) << j)
    return piece


def gather_blocks(block):
    n = lax.axis_size("rows") * lax.axis_size("cols")
    if n > PERMUTE_GROUP_MAX:
        got = lax.all_gather(block, ("rows", "cols"), axis=0, tiled=False)
        order = relative_order(jnp.arange(n, dtype=jnp.int32))
        return jnp.take(got, jnp.argsort(order), axis=0).reshape(-1, block.shape[1])
    return axis_gather(axis_gather(block, "rows"), "cols")


def relative_order(owner):
    n_rows = lax.axis_size("rows")
    n_cols = lax.axis_size("cols")
    return axis_piece("cols", owner % n_cols) * n_rows + axis_piece("rows", owner // n_cols)


def projected_all(all_x, all_sq, centers, centers_sq, residual_b_all, gamma):
    total = all_x.shape[0]
    chunk = min(COLUMN_CHUNK, total)
    if total % chunk != 0:
        chunk = total
    steps = total // chunk

    def piece(start):
        x = lax.dynamic_slice_in_dim(all_x, start, chunk, 0)
        s = lax.dynamic_slice_in_dim(all_sq, start, chunk, 0)
        r = lax.dynamic_slice_in_dim(residual_b_all, start, chunk, 0)
        c = rbf_tile(x, s, centers, centers_sq, gamma)
        return lax.dot_general(c, r, (((0,), (0,)), ((), ())), preferred_element_type=jnp.float32)

    if steps == 1:
        c = lax.optimization_barrier(rbf_tile(all_x, all_sq, centers, centers_sq, gamma))
        return lax.dot_general(
            c, residual_b_all, (((0,), (0,)), ((), ())), preferred_element_type=jnp.float32
        )

    def body(i, acc):
        return acc + piece(i * chunk)

    init = jnp.zeros((centers.shape[0], residual_b_all.shape[1]), jnp.float32)
    return lax.fori_loop(0, steps, body, init)


def local(points, solution, targets, inducing, woodbury_inverse):
    gamma = 2.5 / F
    n_local = points.shape[0]
    n = lax.axis_size("rows") * lax.axis_size("cols")
    me = group_index()
    solution_b = solution.astype(jnp.bfloat16)
    packed = jnp.concatenate([points, solution_b], axis=1)
    gathered = gather_blocks(packed)
    all_x = gathered[:, :F]
    all_v = gathered[:, F:]
    all_sq = square_norms(all_x)
    own_sq = square_norms(points)
    kp = kernel_product(points, own_sq, all_x, all_sq, all_v, gamma)
    residual = targets - kp - noise_level * solution
    owner = inducing // n_local
    position = relative_order(owner) * n_local + inducing % n_local
    centers = jnp.take(all_x, position, axis=0)
    centers_sq = square_norms(centers)
    cross = rbf_tile(points, own_sq, centers, centers_sq, gamma)
    residual_b = residual.astype(jnp.bfloat16)
    res_local = jnp.sum(residual * residual, axis=0)
    tar_local = jnp.sum(targets * targets, axis=0)
    hi, lo = split_bf16(jnp.stack([res_local, tar_local]))
    extra = jnp.zeros((16, residual_b.shape[1]), jnp.bfloat16).at[0:2].set(hi).at[2:4].set(lo)
    sent = jnp.concatenate([residual_b, extra], axis=0)
    got = gather_blocks(sent).reshape(n, sent.shape[0], sent.shape[1])
    residual_b_all = got[:, :n_local].reshape(-1, residual_b.shape[1])
    norm_parts = got[:, n_local:n_local + 2].astype(jnp.float32) + got[:, n_local + 2:n_local + 4].astype(
        jnp.float32
    )
    norms = jnp.sum(norm_parts, axis=0)
    res_sq = norms[0]
    tar_sq = norms[1]
    projected = projected_all(all_x, all_sq, centers, centers_sq, residual_b_all, gamma)
    w_hi, w_lo = split_bf16(woodbury_inverse)
    p_hi, p_lo = split_bf16(projected)
    weights = (
        jnp.dot(w_hi, p_hi, preferred_element_type=jnp.float32)
        + jnp.dot(w_hi, p_lo, preferred_element_type=jnp.float32)
        + jnp.dot(w_lo, p_hi, preferred_element_type=jnp.float32)
    )
    correction = jnp.dot(cross, weights.astype(jnp.bfloat16), preferred_element_type=jnp.float32)
    new_solution = solution + (residual - correction) / noise_level
    relative_norm = jnp.sqrt(res_sq / (tar_sq + 1e-06))
    return (new_solution, residual, relative_norm)


def solution(mesh):
    return jax.shard_map(
        local,
        mesh=mesh,
        in_specs=(
            P(("groups", "rows", "cols"), None),
            P(("groups", "rows", "cols"), None),
            P(("groups", "rows", "cols"), None),
            P("groups"),
            P("groups", None),
        ),
        out_specs=(
            P(("groups", "rows", "cols"), None),
            P(("groups", "rows", "cols"), None),
            P("groups"),
        ),
        check_vma=False,
    )
```

```python
import jax
import jax.numpy as jnp
from jax import lax
from jax.sharding import PartitionSpec as P

F = 128


noise_level = 0.5

COLUMN_CHUNK = 3072


def square_norms(values):
    return jnp.sum(jnp.square(values.astype(jnp.float32)), axis=1)


def rbf_tile(left_x, left_sq, right_x, right_sq, gamma):
    inner = lax.dot_general(
        left_x, right_x, (((1,), (1,)), ((), ())), preferred_element_type=jnp.float32
    )
    return jnp.exp(-gamma * (left_sq[:, None] + right_sq[None, :] - 2.0 * inner)).astype(
        jnp.bfloat16
    )


def kernel_product(own_x, own_sq, all_x, all_sq, all_v, gamma):
    total = all_x.shape[0]
    chunk = min(COLUMN_CHUNK, total)
    if total % chunk != 0:
        chunk = total
    steps = total // chunk

    def piece(start):
        x = lax.dynamic_slice_in_dim(all_x, start, chunk, 0)
        s = lax.dynamic_slice_in_dim(all_sq, start, chunk, 0)
        v = lax.dynamic_slice_in_dim(all_v, start, chunk, 0)
        k = rbf_tile(own_x, own_sq, x, s, gamma)
        return jnp.dot(k, v, preferred_element_type=jnp.float32)

    if steps == 1:
        return piece(0)

    def body(i, acc):
        return acc + piece(i * chunk)

    init = jnp.zeros((own_x.shape[0], all_v.shape[1]), jnp.float32)
    return lax.fori_loop(0, steps, body, init)


def split_bf16(values):
    hi = lax.reduce_precision(values, exponent_bits=8, mantissa_bits=7)
    lo = values - hi
    return hi.astype(jnp.bfloat16), lo.astype(jnp.bfloat16)


PERMUTE_GROUP_MAX = 16


def group_index():
    return lax.axis_index("rows") * lax.axis_size("cols") + lax.axis_index("cols")


def is_power_of_two(n):
    return n & (n - 1) == 0


RING_AXES = ("rows",)


def uses_ring(axis):
    return axis in RING_AXES or not is_power_of_two(lax.axis_size(axis))


def axis_gather(value, axis):
    n = lax.axis_size(axis)
    if uses_ring(axis):
        moved = [value]
        for k in range(1, n):
            perm = [(i, (i + k) % n) for i in range(n)]
            moved.append(lax.ppermute(value, axis, perm))
        return [jnp.concatenate(moved, axis=0)]
    parts = [value]
    bit = n // 2
    while bit >= 1:
        perm = [(i, i ^ bit) for i in range(n)]
        held = parts[0] if len(parts) == 1 else jnp.concatenate(parts, axis=0)
        parts.append(lax.ppermute(held, axis, perm))
        bit //= 2
    return parts


def axis_piece(axis, owner):
    n = lax.axis_size(axis)
    me = lax.axis_index(axis)
    if uses_ring(axis):
        return (me - owner) % n
    d = me ^ owner
    steps = n.bit_length() - 1
    piece = jnp.zeros_like(d)
    for j in range(steps):
        piece = piece + (((d >> (steps - 1 - j)) & 1) << j)
    return piece


def gather_blocks(block):
    n = lax.axis_size("rows") * lax.axis_size("cols")
    if n > PERMUTE_GROUP_MAX:
        got = lax.all_gather(block, ("rows", "cols"), axis=0, tiled=False)
        order = relative_order(jnp.arange(n, dtype=jnp.int32))
        return [jnp.take(got, jnp.argsort(order), axis=0).reshape(-1, block.shape[1])]
    rows_parts = axis_gather(block, "rows")
    return axis_gather(jnp.concatenate(rows_parts, axis=0), "cols")


def relative_order(owner):
    n_rows = lax.axis_size("rows")
    n_cols = lax.axis_size("cols")
    return axis_piece("cols", owner % n_cols) * n_rows + axis_piece("rows", owner // n_cols)


def projected_all(all_x, all_sq, centers, centers_sq, residual_parts, gamma):
    total = all_x.shape[0]
    chunk = min(COLUMN_CHUNK, total)
    if total % chunk != 0:
        chunk = total
    steps = total // chunk
    contract = (((0,), (0,)), ((), ()))

    if steps == 1:
        c = lax.optimization_barrier(rbf_tile(all_x, all_sq, centers, centers_sq, gamma))
        total_p = None
        begin = 0
        for r in residual_parts:
            piece = lax.slice_in_dim(c, begin, begin + r.shape[0], axis=0)
            term = lax.dot_general(piece, r, contract, preferred_element_type=jnp.float32)
            total_p = term if total_p is None else total_p + term
            begin += r.shape[0]
        return total_p

    residual_b_all = jnp.concatenate(residual_parts, axis=0)

    def piece(start):
        x = lax.dynamic_slice_in_dim(all_x, start, chunk, 0)
        s = lax.dynamic_slice_in_dim(all_sq, start, chunk, 0)
        r = lax.dynamic_slice_in_dim(residual_b_all, start, chunk, 0)
        c = rbf_tile(x, s, centers, centers_sq, gamma)
        return lax.dot_general(c, r, contract, preferred_element_type=jnp.float32)

    def body(i, acc):
        return acc + piece(i * chunk)

    init = jnp.zeros((centers.shape[0], residual_b_all.shape[1]), jnp.float32)
    return lax.fori_loop(0, steps, body, init)


def local(points, solution, targets, inducing, woodbury_inverse):
    gamma = 2.5 / F
    n_local = points.shape[0]
    n = lax.axis_size("rows") * lax.axis_size("cols")
    solution_b = solution.astype(jnp.bfloat16)
    packed = jnp.concatenate([points, solution_b], axis=1)
    parts = gather_blocks(packed)
    own_sq = square_norms(points)
    kp = None
    for part in parts:
        part_x = part[:, :F]
        term = kernel_product(points, own_sq, part_x, square_norms(part_x), part[:, F:], gamma)
        kp = term if kp is None else kp + term
    residual = targets - kp - noise_level * solution
    all_x = jnp.concatenate([part[:, :F] for part in parts], axis=0)
    all_sq = square_norms(all_x)
    owner = inducing // n_local
    position = relative_order(owner) * n_local + inducing % n_local
    centers = jnp.take(all_x, position, axis=0)
    centers_sq = square_norms(centers)
    cross = rbf_tile(points, own_sq, centers, centers_sq, gamma)
    residual_b = residual.astype(jnp.bfloat16)
    res_local = jnp.sum(residual * residual, axis=0)
    tar_local = jnp.sum(targets * targets, axis=0)
    hi, lo = split_bf16(jnp.stack([res_local, tar_local]))
    extra = jnp.zeros((16, residual_b.shape[1]), jnp.bfloat16).at[0:2].set(hi).at[2:4].set(lo)
    sent = jnp.concatenate([residual_b, extra], axis=0)
    width = sent.shape[1]
    got_parts = [g.reshape(-1, sent.shape[0], width) for g in gather_blocks(sent)]
    norms = sum(
        jnp.sum(g[:, n_local:n_local + 2].astype(jnp.float32) + g[:, n_local + 2:n_local + 4].astype(jnp.float32), axis=0)
        for g in got_parts
    )
    res_sq = norms[0]
    tar_sq = norms[1]
    residual_parts = [g[:, :n_local].reshape(-1, width) for g in got_parts]
    projected = projected_all(all_x, all_sq, centers, centers_sq, residual_parts, gamma)
    w_hi, w_lo = split_bf16(woodbury_inverse)
    p_hi, p_lo = split_bf16(projected)
    weights = (
        jnp.dot(w_hi, p_hi, preferred_element_type=jnp.float32)
        + jnp.dot(w_hi, p_lo, preferred_element_type=jnp.float32)
        + jnp.dot(w_lo, p_hi, preferred_element_type=jnp.float32)
    )
    correction = jnp.dot(cross, weights.astype(jnp.bfloat16), preferred_element_type=jnp.float32)
    new_solution = solution + (residual - correction) / noise_level
    relative_norm = jnp.sqrt(res_sq / (tar_sq + 1e-06))
    return (new_solution, residual, relative_norm)


def solution(mesh):
    return jax.shard_map(
        local,
        mesh=mesh,
        in_specs=(
            P(("groups", "rows", "cols"), None),
            P(("groups", "rows", "cols"), None),
            P(("groups", "rows", "cols"), None),
            P("groups"),
            P("groups", None),
        ),
        out_specs=(
            P(("groups", "rows", "cols"), None),
            P(("groups", "rows", "cols"), None),
            P("groups"),
        ),
        check_vma=False,
    )
```

```python
import jax
import jax.numpy as jnp
from jax import lax
from jax.sharding import PartitionSpec as P

F = 128


noise_level = 0.5

COLUMN_CHUNK = 3072


def square_norms(values):
    return jnp.sum(jnp.square(values.astype(jnp.float32)), axis=1)


def rbf_tile(left_x, left_sq, right_x, right_sq, gamma):
    inner = lax.dot_general(
        left_x, right_x, (((1,), (1,)), ((), ())), preferred_element_type=jnp.float32
    )
    return jnp.exp(-gamma * (left_sq[:, None] + right_sq[None, :] - 2.0 * inner)).astype(
        jnp.bfloat16
    )


def kernel_product(own_x, own_sq, all_x, all_sq, all_v, gamma):
    total = all_x.shape[0]
    chunk = min(COLUMN_CHUNK, total)
    if total % chunk != 0:
        chunk = total
    steps = total // chunk

    def piece(start):
        x = lax.dynamic_slice_in_dim(all_x, start, chunk, 0)
        s = lax.dynamic_slice_in_dim(all_sq, start, chunk, 0)
        v = lax.dynamic_slice_in_dim(all_v, start, chunk, 0)
        k = rbf_tile(own_x, own_sq, x, s, gamma)
        return jnp.dot(k, v, preferred_element_type=jnp.float32)

    if steps == 1:
        return piece(0)

    def body(i, acc):
        return acc + piece(i * chunk)

    init = jnp.zeros((own_x.shape[0], all_v.shape[1]), jnp.float32)
    return lax.fori_loop(0, steps, body, init)


def split_bf16(values):
    hi = lax.reduce_precision(values, exponent_bits=8, mantissa_bits=7)
    lo = values - hi
    return hi.astype(jnp.bfloat16), lo.astype(jnp.bfloat16)


PERMUTE_GROUP_MAX = 16


def group_index():
    return lax.axis_index("rows") * lax.axis_size("cols") + lax.axis_index("cols")


def is_power_of_two(n):
    return n & (n - 1) == 0


RING_AXES = ("rows",)


def uses_ring(axis):
    return axis in RING_AXES or not is_power_of_two(lax.axis_size(axis))


def axis_gather(value, axis):
    n = lax.axis_size(axis)
    if uses_ring(axis):
        moved = [value]
        for k in range(1, n):
            perm = [(i, (i + k) % n) for i in range(n)]
            moved.append(lax.ppermute(value, axis, perm))
        return [jnp.concatenate(moved, axis=0)]
    parts = [value]
    bit = n // 2
    while bit >= 1:
        perm = [(i, i ^ bit) for i in range(n)]
        held = parts[0] if len(parts) == 1 else jnp.concatenate(parts, axis=0)
        parts.append(lax.ppermute(held, axis, perm))
        bit //= 2
    return parts


def axis_piece(axis, owner):
    n = lax.axis_size(axis)
    me = lax.axis_index(axis)
    if uses_ring(axis):
        return (me - owner) % n
    d = me ^ owner
    steps = n.bit_length() - 1
    piece = jnp.zeros_like(d)
    for j in range(steps):
        piece = piece + (((d >> (steps - 1 - j)) & 1) << j)
    return piece


def gather_blocks(block):
    n = lax.axis_size("rows") * lax.axis_size("cols")
    if n > PERMUTE_GROUP_MAX:
        got = lax.all_gather(block, ("rows", "cols"), axis=0, tiled=False)
        order = relative_order(jnp.arange(n, dtype=jnp.int32))
        return [jnp.take(got, jnp.argsort(order), axis=0).reshape(-1, block.shape[1])]
    if not uses_ring("rows") or uses_ring("cols"):
        return axis_gather(jnp.concatenate(axis_gather(block, "rows"), axis=0), "cols")
    return early_flip_gather(block)


def early_flip_gather(block):
    n_rows = lax.axis_size("rows")
    n_cols = lax.axis_size("cols")
    ring = [lax.ppermute(block, "rows", [(i, (i + k) % n_rows) for i in range(n_rows)]) for k in range(1, n_rows)]
    bit = n_cols // 2
    flip = [(i, i ^ bit) for i in range(n_cols)]
    own_flipped = lax.ppermute(block, "cols", flip)
    ring_flipped = lax.ppermute(jnp.concatenate(ring, axis=0), "cols", flip)
    parts = [block] + ring + [own_flipped, ring_flipped]
    bit //= 2
    while bit >= 1:
        perm = [(i, i ^ bit) for i in range(n_cols)]
        parts.append(lax.ppermute(jnp.concatenate(parts, axis=0), "cols", perm))
        bit //= 2
    return parts


def relative_order(owner):
    n_rows = lax.axis_size("rows")
    n_cols = lax.axis_size("cols")
    return axis_piece("cols", owner % n_cols) * n_rows + axis_piece("rows", owner // n_cols)


def projected_all(all_x, all_sq, centers, centers_sq, residual_parts, gamma):
    total = all_x.shape[0]
    chunk = min(COLUMN_CHUNK, total)
    if total % chunk != 0:
        chunk = total
    steps = total // chunk
    contract = (((0,), (0,)), ((), ()))

    if steps == 1:
        c = lax.optimization_barrier(rbf_tile(all_x, all_sq, centers, centers_sq, gamma))
        total_p = None
        begin = 0
        for r in residual_parts:
            piece = lax.slice_in_dim(c, begin, begin + r.shape[0], axis=0)
            term = lax.dot_general(piece, r, contract, preferred_element_type=jnp.float32)
            total_p = term if total_p is None else total_p + term
            begin += r.shape[0]
        return total_p

    residual_b_all = jnp.concatenate(residual_parts, axis=0)

    def piece(start):
        x = lax.dynamic_slice_in_dim(all_x, start, chunk, 0)
        s = lax.dynamic_slice_in_dim(all_sq, start, chunk, 0)
        r = lax.dynamic_slice_in_dim(residual_b_all, start, chunk, 0)
        c = rbf_tile(x, s, centers, centers_sq, gamma)
        return lax.dot_general(c, r, contract, preferred_element_type=jnp.float32)

    def body(i, acc):
        return acc + piece(i * chunk)

    init = jnp.zeros((centers.shape[0], residual_b_all.shape[1]), jnp.float32)
    return lax.fori_loop(0, steps, body, init)


def local(points, solution, targets, inducing, woodbury_inverse):
    gamma = 2.5 / F
    n_local = points.shape[0]
    n = lax.axis_size("rows") * lax.axis_size("cols")
    solution_b = solution.astype(jnp.bfloat16)
    packed = jnp.concatenate([points, solution_b], axis=1)
    parts = gather_blocks(packed)
    own_sq = square_norms(points)
    kp = None
    for part in parts:
        part_x = part[:, :F]
        term = kernel_product(points, own_sq, part_x, square_norms(part_x), part[:, F:], gamma)
        kp = term if kp is None else kp + term
    residual = targets - kp - noise_level * solution
    all_x = jnp.concatenate([part[:, :F] for part in parts], axis=0)
    all_sq = square_norms(all_x)
    owner = inducing // n_local
    position = relative_order(owner) * n_local + inducing % n_local
    centers = jnp.take(all_x, position, axis=0)
    centers_sq = square_norms(centers)
    cross = rbf_tile(points, own_sq, centers, centers_sq, gamma)
    residual_b = residual.astype(jnp.bfloat16)
    res_local = jnp.sum(residual * residual, axis=0)
    tar_local = jnp.sum(targets * targets, axis=0)
    hi, lo = split_bf16(jnp.stack([res_local, tar_local]))
    extra = jnp.zeros((16, residual_b.shape[1]), jnp.bfloat16).at[0:2].set(hi).at[2:4].set(lo)
    sent = jnp.concatenate([residual_b, extra], axis=0)
    width = sent.shape[1]
    got_parts = [g.reshape(-1, sent.shape[0], width) for g in gather_blocks(sent)]
    norms = sum(
        jnp.sum(g[:, n_local:n_local + 2].astype(jnp.float32) + g[:, n_local + 2:n_local + 4].astype(jnp.float32), axis=0)
        for g in got_parts
    )
    res_sq = norms[0]
    tar_sq = norms[1]
    residual_parts = [g[:, :n_local].reshape(-1, width) for g in got_parts]
    projected = projected_all(all_x, all_sq, centers, centers_sq, residual_parts, gamma)
    w_hi, w_lo = split_bf16(woodbury_inverse)
    p_hi, p_lo = split_bf16(projected)
    both = jnp.dot(w_hi, jnp.concatenate([p_hi, p_lo], axis=1), preferred_element_type=jnp.float32)
    r = p_hi.shape[1]
    weights = both[:, :r] + both[:, r:] + jnp.dot(w_lo, p_hi, preferred_element_type=jnp.float32)
    correction = jnp.dot(cross, weights.astype(jnp.bfloat16), preferred_element_type=jnp.float32)
    new_solution = solution + (residual - correction) / noise_level
    relative_norm = jnp.sqrt(res_sq / (tar_sq + 1e-06))
    return (new_solution, residual, relative_norm)


def solution(mesh):
    return jax.shard_map(
        local,
        mesh=mesh,
        in_specs=(
            P(("groups", "rows", "cols"), None),
            P(("groups", "rows", "cols"), None),
            P(("groups", "rows", "cols"), None),
            P("groups"),
            P("groups", None),
        ),
        out_specs=(
            P(("groups", "rows", "cols"), None),
            P(("groups", "rows", "cols"), None),
            P("groups"),
        ),
        check_vma=False,
    )
```

```python
import jax
import jax.numpy as jnp
from jax import lax
from jax.sharding import PartitionSpec as P

F = 128


noise_level = 0.5

COLUMN_CHUNK = 3072


def square_norms(values):
    return jnp.sum(jnp.square(values.astype(jnp.float32)), axis=1)


def rbf_tile(left_x, left_sq, right_x, right_sq, gamma):
    inner = lax.dot_general(
        left_x, right_x, (((1,), (1,)), ((), ())), preferred_element_type=jnp.float32
    )
    return jnp.exp(-gamma * (left_sq[:, None] + right_sq[None, :] - 2.0 * inner)).astype(
        jnp.bfloat16
    )


def kernel_product(own_x, own_sq, all_x, all_sq, all_v, gamma):
    total = all_x.shape[0]
    chunk = min(COLUMN_CHUNK, total)
    if total % chunk != 0:
        chunk = total
    steps = total // chunk

    def piece(start):
        x = lax.dynamic_slice_in_dim(all_x, start, chunk, 0)
        s = lax.dynamic_slice_in_dim(all_sq, start, chunk, 0)
        v = lax.dynamic_slice_in_dim(all_v, start, chunk, 0)
        k = rbf_tile(own_x, own_sq, x, s, gamma)
        return jnp.dot(k, v, preferred_element_type=jnp.float32)

    if steps == 1:
        return piece(0)

    def body(i, acc):
        return acc + piece(i * chunk)

    init = jnp.zeros((own_x.shape[0], all_v.shape[1]), jnp.float32)
    return lax.fori_loop(0, steps, body, init)


def split_bf16(values):
    hi = lax.reduce_precision(values, exponent_bits=8, mantissa_bits=7)
    lo = values - hi
    return hi.astype(jnp.bfloat16), lo.astype(jnp.bfloat16)


PERMUTE_GROUP_MAX = 16


def group_index():
    return lax.axis_index("rows") * lax.axis_size("cols") + lax.axis_index("cols")


def is_power_of_two(n):
    return n & (n - 1) == 0


RING_AXES = ("rows",)


def uses_ring(axis):
    return axis in RING_AXES or not is_power_of_two(lax.axis_size(axis))


def axis_gather(value, axis):
    n = lax.axis_size(axis)
    if uses_ring(axis):
        moved = [value]
        for k in range(1, n):
            perm = [(i, (i + k) % n) for i in range(n)]
            moved.append(lax.ppermute(value, axis, perm))
        return [jnp.concatenate(moved, axis=0)]
    parts = [value]
    bit = n // 2
    while bit >= 1:
        perm = [(i, i ^ bit) for i in range(n)]
        held = parts[0] if len(parts) == 1 else jnp.concatenate(parts, axis=0)
        parts.append(lax.ppermute(held, axis, perm))
        bit //= 2
    return parts


def axis_piece(axis, owner):
    n = lax.axis_size(axis)
    me = lax.axis_index(axis)
    if uses_ring(axis):
        return (me - owner) % n
    d = me ^ owner
    steps = n.bit_length() - 1
    piece = jnp.zeros_like(d)
    for j in range(steps):
        piece = piece + (((d >> (steps - 1 - j)) & 1) << j)
    return piece


def gather_blocks(block, early_flip=False):
    n = lax.axis_size("rows") * lax.axis_size("cols")
    if n > PERMUTE_GROUP_MAX:
        got = lax.all_gather(block, ("rows", "cols"), axis=0, tiled=False)
        order = relative_order(jnp.arange(n, dtype=jnp.int32))
        return [jnp.take(got, jnp.argsort(order), axis=0).reshape(-1, block.shape[1])]
    if not early_flip or not uses_ring("rows") or uses_ring("cols"):
        return axis_gather(jnp.concatenate(axis_gather(block, "rows"), axis=0), "cols")
    return early_flip_gather(block)


def early_flip_gather(block):
    n_rows = lax.axis_size("rows")
    n_cols = lax.axis_size("cols")
    ring = [lax.ppermute(block, "rows", [(i, (i + k) % n_rows) for i in range(n_rows)]) for k in range(1, n_rows)]
    bit = n_cols // 2
    flip = [(i, i ^ bit) for i in range(n_cols)]
    own_flipped = lax.ppermute(block, "cols", flip)
    ring_flipped = lax.ppermute(jnp.concatenate(ring, axis=0), "cols", flip)
    parts = [block] + ring + [own_flipped, ring_flipped]
    bit //= 2
    while bit >= 1:
        perm = [(i, i ^ bit) for i in range(n_cols)]
        parts.append(lax.ppermute(jnp.concatenate(parts, axis=0), "cols", perm))
        bit //= 2
    return parts


def relative_order(owner):
    n_rows = lax.axis_size("rows")
    n_cols = lax.axis_size("cols")
    return axis_piece("cols", owner % n_cols) * n_rows + axis_piece("rows", owner // n_cols)


def projected_all(all_x, all_sq, centers, centers_sq, residual_parts, gamma):
    total = all_x.shape[0]
    chunk = min(COLUMN_CHUNK, total)
    if total % chunk != 0:
        chunk = total
    steps = total // chunk
    contract = (((0,), (0,)), ((), ()))

    if steps == 1:
        c = lax.optimization_barrier(rbf_tile(all_x, all_sq, centers, centers_sq, gamma))
        total_p = None
        begin = 0
        for r in residual_parts:
            piece = lax.slice_in_dim(c, begin, begin + r.shape[0], axis=0)
            term = lax.dot_general(piece, r, contract, preferred_element_type=jnp.float32)
            total_p = term if total_p is None else total_p + term
            begin += r.shape[0]
        return total_p

    residual_b_all = jnp.concatenate(residual_parts, axis=0)

    def piece(start):
        x = lax.dynamic_slice_in_dim(all_x, start, chunk, 0)
        s = lax.dynamic_slice_in_dim(all_sq, start, chunk, 0)
        r = lax.dynamic_slice_in_dim(residual_b_all, start, chunk, 0)
        c = rbf_tile(x, s, centers, centers_sq, gamma)
        return lax.dot_general(c, r, contract, preferred_element_type=jnp.float32)

    def body(i, acc):
        return acc + piece(i * chunk)

    init = jnp.zeros((centers.shape[0], residual_b_all.shape[1]), jnp.float32)
    return lax.fori_loop(0, steps, body, init)


def local(points, solution, targets, inducing, woodbury_inverse):
    gamma = 2.5 / F
    n_local = points.shape[0]
    n = lax.axis_size("rows") * lax.axis_size("cols")
    solution_b = solution.astype(jnp.bfloat16)
    packed = jnp.concatenate([points, solution_b], axis=1)
    parts = gather_blocks(packed, early_flip=True)
    own_sq = square_norms(points)
    kp = None
    for part in parts:
        part_x = part[:, :F]
        term = kernel_product(points, own_sq, part_x, square_norms(part_x), part[:, F:], gamma)
        kp = term if kp is None else kp + term
    residual = targets - kp - noise_level * solution
    all_x = jnp.concatenate([part[:, :F] for part in parts], axis=0)
    all_sq = square_norms(all_x)
    owner = inducing // n_local
    position = relative_order(owner) * n_local + inducing % n_local
    centers = jnp.take(all_x, position, axis=0)
    centers_sq = square_norms(centers)
    cross = rbf_tile(points, own_sq, centers, centers_sq, gamma)
    residual_b = residual.astype(jnp.bfloat16)
    res_local = jnp.sum(residual * residual, axis=0)
    tar_local = jnp.sum(targets * targets, axis=0)
    hi, lo = split_bf16(jnp.stack([res_local, tar_local]))
    extra = jnp.zeros((16, residual_b.shape[1]), jnp.bfloat16).at[0:2].set(hi).at[2:4].set(lo)
    sent = jnp.concatenate([residual_b, extra], axis=0)
    width = sent.shape[1]
    got_parts = [g.reshape(-1, sent.shape[0], width) for g in gather_blocks(sent)]
    norms = sum(
        jnp.sum(g[:, n_local:n_local + 2].astype(jnp.float32) + g[:, n_local + 2:n_local + 4].astype(jnp.float32), axis=0)
        for g in got_parts
    )
    res_sq = norms[0]
    tar_sq = norms[1]
    residual_parts = [g[:, :n_local].reshape(-1, width) for g in got_parts]
    projected = projected_all(all_x, all_sq, centers, centers_sq, residual_parts, gamma)
    w_hi, w_lo = split_bf16(woodbury_inverse)
    p_hi, p_lo = split_bf16(projected)
    weights = (
        jnp.dot(w_hi, p_hi, preferred_element_type=jnp.float32)
        + jnp.dot(w_hi, p_lo, preferred_element_type=jnp.float32)
        + jnp.dot(w_lo, p_hi, preferred_element_type=jnp.float32)
    )
    correction = jnp.dot(cross, weights.astype(jnp.bfloat16), preferred_element_type=jnp.float32)
    new_solution = solution + (residual - correction) / noise_level
    relative_norm = jnp.sqrt(res_sq / (tar_sq + 1e-06))
    return (new_solution, residual, relative_norm)


def solution(mesh):
    return jax.shard_map(
        local,
        mesh=mesh,
        in_specs=(
            P(("groups", "rows", "cols"), None),
            P(("groups", "rows", "cols"), None),
            P(("groups", "rows", "cols"), None),
            P("groups"),
            P("groups", None),
        ),
        out_specs=(
            P(("groups", "rows", "cols"), None),
            P(("groups", "rows", "cols"), None),
            P("groups"),
        ),
        check_vma=False,
    )
```

```python
import jax
import jax.numpy as jnp
from jax import lax
from jax.sharding import PartitionSpec as P

F = 128


noise_level = 0.5

COLUMN_CHUNK = 3072


def square_norms(values):
    return jnp.sum(jnp.square(values.astype(jnp.float32)), axis=1)


def rbf_tile(left_x, left_sq, right_x, right_sq, gamma):
    inner = lax.dot_general(
        left_x, right_x, (((1,), (1,)), ((), ())), preferred_element_type=jnp.float32
    )
    return jnp.exp(-gamma * (left_sq[:, None] + right_sq[None, :] - 2.0 * inner)).astype(
        jnp.bfloat16
    )


def kernel_product(own_x, own_sq, all_x, all_sq, all_v, gamma):
    total = all_x.shape[0]
    chunk = min(COLUMN_CHUNK, total)
    if total % chunk != 0:
        chunk = total
    steps = total // chunk

    def piece(start):
        x = lax.dynamic_slice_in_dim(all_x, start, chunk, 0)
        s = lax.dynamic_slice_in_dim(all_sq, start, chunk, 0)
        v = lax.dynamic_slice_in_dim(all_v, start, chunk, 0)
        k = rbf_tile(own_x, own_sq, x, s, gamma)
        return jnp.dot(k, v, preferred_element_type=jnp.float32)

    if steps == 1:
        return piece(0)

    def body(i, acc):
        return acc + piece(i * chunk)

    init = jnp.zeros((own_x.shape[0], all_v.shape[1]), jnp.float32)
    return lax.fori_loop(0, steps, body, init)


def split_bf16(values):
    hi = lax.reduce_precision(values, exponent_bits=8, mantissa_bits=7)
    lo = values - hi
    return hi.astype(jnp.bfloat16), lo.astype(jnp.bfloat16)


PERMUTE_GROUP_MAX = 16


def group_index():
    return lax.axis_index("rows") * lax.axis_size("cols") + lax.axis_index("cols")


def is_power_of_two(n):
    return n & (n - 1) == 0


RING_AXES = ("rows",)


def uses_ring(axis):
    return axis in RING_AXES or not is_power_of_two(lax.axis_size(axis))


def axis_gather(value, axis):
    n = lax.axis_size(axis)
    if uses_ring(axis):
        moved = [value]
        for k in range(1, n):
            perm = [(i, (i + k) % n) for i in range(n)]
            moved.append(lax.ppermute(value, axis, perm))
        return [jnp.concatenate(moved, axis=0)]
    parts = [value]
    bit = n // 2
    while bit >= 1:
        perm = [(i, i ^ bit) for i in range(n)]
        held = parts[0] if len(parts) == 1 else jnp.concatenate(parts, axis=0)
        parts.append(lax.ppermute(held, axis, perm))
        bit //= 2
    return parts


def axis_piece(axis, owner):
    n = lax.axis_size(axis)
    me = lax.axis_index(axis)
    if uses_ring(axis):
        return (me - owner) % n
    d = me ^ owner
    steps = n.bit_length() - 1
    piece = jnp.zeros_like(d)
    for j in range(steps):
        piece = piece + (((d >> (steps - 1 - j)) & 1) << j)
    return piece


def gather_blocks(block, early_flip=False):
    n = lax.axis_size("rows") * lax.axis_size("cols")
    if n > PERMUTE_GROUP_MAX:
        got = lax.all_gather(block, ("rows", "cols"), axis=0, tiled=False)
        order = relative_order(jnp.arange(n, dtype=jnp.int32))
        return [jnp.take(got, jnp.argsort(order), axis=0).reshape(-1, block.shape[1])]
    if not uses_ring("rows") or uses_ring("cols"):
        return axis_gather(jnp.concatenate(axis_gather(block, "rows"), axis=0), "cols")
    n_rows = lax.axis_size("rows")
    ring = [lax.ppermute(block, "rows", [(i, (i + k) % n_rows) for i in range(n_rows)]) for k in range(1, n_rows)]
    if early_flip:
        parts = [block, jnp.concatenate(ring, axis=0)]
    else:
        parts = [jnp.concatenate([block] + ring, axis=0)]
    return pipelined_xor_gather(parts, "cols")


def pipelined_xor_gather(parts, axis):
    n = lax.axis_size(axis)
    bit = n // 2
    while bit >= 1:
        perm = [(i, i ^ bit) for i in range(n)]
        if len(parts) == 1:
            sends = parts
        else:
            sends = [jnp.concatenate(parts[:-1], axis=0), parts[-1]]
        parts = parts + [lax.ppermute(p, axis, perm) for p in sends]
        bit //= 2
    return parts


def relative_order(owner):
    n_rows = lax.axis_size("rows")
    n_cols = lax.axis_size("cols")
    return axis_piece("cols", owner % n_cols) * n_rows + axis_piece("rows", owner // n_cols)


def projected_all(all_x, all_sq, centers, centers_sq, residual_parts, gamma):
    total = all_x.shape[0]
    chunk = min(COLUMN_CHUNK, total)
    if total % chunk != 0:
        chunk = total
    steps = total // chunk
    contract = (((0,), (0,)), ((), ()))

    if steps == 1:
        c = lax.optimization_barrier(rbf_tile(all_x, all_sq, centers, centers_sq, gamma))
        total_p = None
        begin = 0
        for r in residual_parts:
            piece = lax.slice_in_dim(c, begin, begin + r.shape[0], axis=0)
            term = lax.dot_general(piece, r, contract, preferred_element_type=jnp.float32)
            total_p = term if total_p is None else total_p + term
            begin += r.shape[0]
        return total_p

    residual_b_all = jnp.concatenate(residual_parts, axis=0)

    def piece(start):
        x = lax.dynamic_slice_in_dim(all_x, start, chunk, 0)
        s = lax.dynamic_slice_in_dim(all_sq, start, chunk, 0)
        r = lax.dynamic_slice_in_dim(residual_b_all, start, chunk, 0)
        c = rbf_tile(x, s, centers, centers_sq, gamma)
        return lax.dot_general(c, r, contract, preferred_element_type=jnp.float32)

    def body(i, acc):
        return acc + piece(i * chunk)

    init = jnp.zeros((centers.shape[0], residual_b_all.shape[1]), jnp.float32)
    return lax.fori_loop(0, steps, body, init)


def local(points, solution, targets, inducing, woodbury_inverse):
    gamma = 2.5 / F
    n_local = points.shape[0]
    n = lax.axis_size("rows") * lax.axis_size("cols")
    solution_b = solution.astype(jnp.bfloat16)
    packed = jnp.concatenate([points, solution_b], axis=1)
    parts = gather_blocks(packed, early_flip=True)
    own_sq = square_norms(points)
    kp = None
    for part in parts:
        part_x = part[:, :F]
        term = kernel_product(points, own_sq, part_x, square_norms(part_x), part[:, F:], gamma)
        kp = term if kp is None else kp + term
    residual = targets - kp - noise_level * solution
    all_x = jnp.concatenate([part[:, :F] for part in parts], axis=0)
    all_sq = square_norms(all_x)
    owner = inducing // n_local
    position = relative_order(owner) * n_local + inducing % n_local
    centers = jnp.take(all_x, position, axis=0)
    centers_sq = square_norms(centers)
    cross = rbf_tile(points, own_sq, centers, centers_sq, gamma)
    residual_b = residual.astype(jnp.bfloat16)
    res_local = jnp.sum(residual * residual, axis=0)
    tar_local = jnp.sum(targets * targets, axis=0)
    hi, lo = split_bf16(jnp.stack([res_local, tar_local]))
    extra = jnp.zeros((16, residual_b.shape[1]), jnp.bfloat16).at[0:2].set(hi).at[2:4].set(lo)
    sent = jnp.concatenate([residual_b, extra], axis=0)
    width = sent.shape[1]
    got_parts = [g.reshape(-1, sent.shape[0], width) for g in gather_blocks(sent)]
    norms = sum(
        jnp.sum(g[:, n_local:n_local + 2].astype(jnp.float32) + g[:, n_local + 2:n_local + 4].astype(jnp.float32), axis=0)
        for g in got_parts
    )
    res_sq = norms[0]
    tar_sq = norms[1]
    residual_parts = [g[:, :n_local].reshape(-1, width) for g in got_parts]
    projected = projected_all(all_x, all_sq, centers, centers_sq, residual_parts, gamma)
    w_hi, w_lo = split_bf16(woodbury_inverse)
    p_hi, p_lo = split_bf16(projected)
    weights = (
        jnp.dot(w_hi, p_hi, preferred_element_type=jnp.float32)
        + jnp.dot(w_hi, p_lo, preferred_element_type=jnp.float32)
        + jnp.dot(w_lo, p_hi, preferred_element_type=jnp.float32)
    )
    correction = jnp.dot(cross, weights.astype(jnp.bfloat16), preferred_element_type=jnp.float32)
    new_solution = solution + (residual - correction) / noise_level
    relative_norm = jnp.sqrt(res_sq / (tar_sq + 1e-06))
    return (new_solution, residual, relative_norm)


def solution(mesh):
    return jax.shard_map(
        local,
        mesh=mesh,
        in_specs=(
            P(("groups", "rows", "cols"), None),
            P(("groups", "rows", "cols"), None),
            P(("groups", "rows", "cols"), None),
            P("groups"),
            P("groups", None),
        ),
        out_specs=(
            P(("groups", "rows", "cols"), None),
            P(("groups", "rows", "cols"), None),
            P("groups"),
        ),
        check_vma=False,
    )
```

```python
import jax
import jax.numpy as jnp
from jax import lax
from jax.sharding import PartitionSpec as P

F = 128


noise_level = 0.5

COLUMN_CHUNK = 3072


def square_norms(values):
    return jnp.sum(jnp.square(values.astype(jnp.float32)), axis=1)


def rbf_tile(left_x, left_sq, right_x, right_sq, gamma):
    inner = lax.dot_general(
        left_x, right_x, (((1,), (1,)), ((), ())), preferred_element_type=jnp.float32
    )
    return jnp.exp(-gamma * (left_sq[:, None] + right_sq[None, :] - 2.0 * inner)).astype(
        jnp.bfloat16
    )


def kernel_product(own_x, own_sq, all_x, all_sq, all_v, gamma):
    total = all_x.shape[0]
    chunk = min(COLUMN_CHUNK, total)
    if total % chunk != 0:
        chunk = total
    steps = total // chunk

    def piece(start):
        x = lax.dynamic_slice_in_dim(all_x, start, chunk, 0)
        s = lax.dynamic_slice_in_dim(all_sq, start, chunk, 0)
        v = lax.dynamic_slice_in_dim(all_v, start, chunk, 0)
        k = rbf_tile(own_x, own_sq, x, s, gamma)
        return jnp.dot(k, v, preferred_element_type=jnp.float32)

    if steps == 1:
        return piece(0)

    def body(i, acc):
        return acc + piece(i * chunk)

    init = jnp.zeros((own_x.shape[0], all_v.shape[1]), jnp.float32)
    return lax.fori_loop(0, steps, body, init)


def split_bf16(values):
    hi = lax.reduce_precision(values, exponent_bits=8, mantissa_bits=7)
    lo = values - hi
    return hi.astype(jnp.bfloat16), lo.astype(jnp.bfloat16)


PERMUTE_GROUP_MAX = 16


def group_index():
    return lax.axis_index("rows") * lax.axis_size("cols") + lax.axis_index("cols")


def is_power_of_two(n):
    return n & (n - 1) == 0


RING_AXES = ("rows",)


def uses_ring(axis):
    return axis in RING_AXES or not is_power_of_two(lax.axis_size(axis))


def axis_gather(value, axis):
    n = lax.axis_size(axis)
    if uses_ring(axis):
        moved = [value]
        for k in range(1, n):
            perm = [(i, (i + k) % n) for i in range(n)]
            moved.append(lax.ppermute(value, axis, perm))
        return [jnp.concatenate(moved, axis=0)]
    parts = [value]
    bit = n // 2
    while bit >= 1:
        perm = [(i, i ^ bit) for i in range(n)]
        held = parts[0] if len(parts) == 1 else jnp.concatenate(parts, axis=0)
        parts.append(lax.ppermute(held, axis, perm))
        bit //= 2
    return parts


def axis_piece(axis, owner):
    n = lax.axis_size(axis)
    me = lax.axis_index(axis)
    if uses_ring(axis):
        return (me - owner) % n
    d = me ^ owner
    steps = n.bit_length() - 1
    piece = jnp.zeros_like(d)
    for j in range(steps):
        piece = piece + (((d >> (steps - 1 - j)) & 1) << j)
    return piece


def gather_blocks(block, early_flip=False):
    n = lax.axis_size("rows") * lax.axis_size("cols")
    if n > PERMUTE_GROUP_MAX:
        got = lax.all_gather(block, ("rows", "cols"), axis=0, tiled=False)
        order = relative_order(jnp.arange(n, dtype=jnp.int32))
        return [jnp.take(got, jnp.argsort(order), axis=0).reshape(-1, block.shape[1])]
    if not uses_ring("rows") or uses_ring("cols"):
        return axis_gather(jnp.concatenate(axis_gather(block, "rows"), axis=0), "cols")
    n_rows = lax.axis_size("rows")
    ring = [lax.ppermute(block, "rows", [(i, (i + k) % n_rows) for i in range(n_rows)]) for k in range(1, n_rows)]
    if early_flip:
        return pipelined_xor_gather([block, jnp.concatenate(ring, axis=0)], "cols")
    return axis_gather(jnp.concatenate([block] + ring, axis=0), "cols")


def pipelined_xor_gather(parts, axis):
    n = lax.axis_size(axis)
    bit = n // 2
    while bit >= 1:
        perm = [(i, i ^ bit) for i in range(n)]
        if len(parts) == 1:
            sends = parts
        else:
            sends = [jnp.concatenate(parts[:-1], axis=0), parts[-1]]
        parts = parts + [lax.ppermute(p, axis, perm) for p in sends]
        bit //= 2
    return parts


def relative_order(owner):
    n_rows = lax.axis_size("rows")
    n_cols = lax.axis_size("cols")
    return axis_piece("cols", owner % n_cols) * n_rows + axis_piece("rows", owner // n_cols)


def projected_all(all_x, all_sq, centers, centers_sq, residual_parts, gamma):
    total = all_x.shape[0]
    chunk = min(COLUMN_CHUNK, total)
    if total % chunk != 0:
        chunk = total
    steps = total // chunk
    contract = (((0,), (0,)), ((), ()))

    if steps == 1:
        c = lax.optimization_barrier(rbf_tile(all_x, all_sq, centers, centers_sq, gamma))
        total_p = None
        begin = 0
        for r in residual_parts:
            piece = lax.slice_in_dim(c, begin, begin + r.shape[0], axis=0)
            term = lax.dot_general(piece, r, contract, preferred_element_type=jnp.float32)
            total_p = term if total_p is None else total_p + term
            begin += r.shape[0]
        return total_p

    residual_b_all = jnp.concatenate(residual_parts, axis=0)

    def piece(start):
        x = lax.dynamic_slice_in_dim(all_x, start, chunk, 0)
        s = lax.dynamic_slice_in_dim(all_sq, start, chunk, 0)
        r = lax.dynamic_slice_in_dim(residual_b_all, start, chunk, 0)
        c = rbf_tile(x, s, centers, centers_sq, gamma)
        return lax.dot_general(c, r, contract, preferred_element_type=jnp.float32)

    def body(i, acc):
        return acc + piece(i * chunk)

    init = jnp.zeros((centers.shape[0], residual_b_all.shape[1]), jnp.float32)
    return lax.fori_loop(0, steps, body, init)


def local(points, solution, targets, inducing, woodbury_inverse):
    gamma = 2.5 / F
    n_local = points.shape[0]
    n = lax.axis_size("rows") * lax.axis_size("cols")
    solution_b = solution.astype(jnp.bfloat16)
    packed = jnp.concatenate([points, solution_b], axis=1)
    parts = gather_blocks(packed, early_flip=True)
    own_sq = square_norms(points)
    kp = None
    for part in parts:
        part_x = part[:, :F]
        term = kernel_product(points, own_sq, part_x, square_norms(part_x), part[:, F:], gamma)
        kp = term if kp is None else kp + term
    residual = targets - kp - noise_level * solution
    all_x = jnp.concatenate([part[:, :F] for part in parts], axis=0)
    all_sq = square_norms(all_x)
    owner = inducing // n_local
    position = relative_order(owner) * n_local + inducing % n_local
    centers = jnp.take(all_x, position, axis=0)
    centers_sq = square_norms(centers)
    cross = rbf_tile(points, own_sq, centers, centers_sq, gamma)
    residual_b = residual.astype(jnp.bfloat16)
    res_local = jnp.sum(residual * residual, axis=0)
    tar_local = jnp.sum(targets * targets, axis=0)
    hi, lo = split_bf16(jnp.stack([res_local, tar_local]))
    extra = jnp.zeros((16, residual_b.shape[1]), jnp.bfloat16).at[0:2].set(hi).at[2:4].set(lo)
    sent = jnp.concatenate([residual_b, extra], axis=0)
    width = sent.shape[1]
    got_parts = [g.reshape(-1, sent.shape[0], width) for g in gather_blocks(sent)]
    norms = sum(
        jnp.sum(g[:, n_local:n_local + 2].astype(jnp.float32) + g[:, n_local + 2:n_local + 4].astype(jnp.float32), axis=0)
        for g in got_parts
    )
    res_sq = norms[0]
    tar_sq = norms[1]
    residual_parts = [g[:, :n_local].reshape(-1, width) for g in got_parts]
    projected = projected_all(all_x, all_sq, centers, centers_sq, residual_parts, gamma)
    w_hi, w_lo = split_bf16(woodbury_inverse)
    p_hi, p_lo = split_bf16(projected)
    weights = (
        jnp.dot(w_hi, p_hi, preferred_element_type=jnp.float32)
        + jnp.dot(w_hi, p_lo, preferred_element_type=jnp.float32)
        + jnp.dot(w_lo, p_hi, preferred_element_type=jnp.float32)
    )
    correction = jnp.dot(cross, weights.astype(jnp.bfloat16), preferred_element_type=jnp.float32)
    new_solution = solution + (residual - correction) / noise_level
    relative_norm = jnp.sqrt(res_sq / (tar_sq + 1e-06))
    return (new_solution, residual, relative_norm)


def solution(mesh):
    return jax.shard_map(
        local,
        mesh=mesh,
        in_specs=(
            P(("groups", "rows", "cols"), None),
            P(("groups", "rows", "cols"), None),
            P(("groups", "rows", "cols"), None),
            P("groups"),
            P("groups", None),
        ),
        out_specs=(
            P(("groups", "rows", "cols"), None),
            P(("groups", "rows", "cols"), None),
            P("groups"),
        ),
        check_vma=False,
    )
```

```python
import jax
import jax.numpy as jnp
from jax import lax
from jax.sharding import PartitionSpec as P

F = 128


noise_level = 0.5

COLUMN_CHUNK = 3072


def square_norms(values):
    return jnp.sum(jnp.square(values.astype(jnp.float32)), axis=1)


def rbf_tile(left_x, left_sq, right_x, right_sq, gamma):
    inner = lax.dot_general(
        left_x, right_x, (((1,), (1,)), ((), ())), preferred_element_type=jnp.float32
    )
    return jnp.exp(-gamma * (left_sq[:, None] + right_sq[None, :] - 2.0 * inner)).astype(
        jnp.bfloat16
    )


def kernel_product(own_x, own_sq, all_x, all_sq, all_v, gamma):
    total = all_x.shape[0]
    chunk = min(COLUMN_CHUNK, total)
    if total % chunk != 0:
        chunk = total
    steps = total // chunk

    def piece(start):
        x = lax.dynamic_slice_in_dim(all_x, start, chunk, 0)
        s = lax.dynamic_slice_in_dim(all_sq, start, chunk, 0)
        v = lax.dynamic_slice_in_dim(all_v, start, chunk, 0)
        k = rbf_tile(own_x, own_sq, x, s, gamma)
        return jnp.dot(k, v, preferred_element_type=jnp.float32)

    if steps == 1:
        return piece(0)

    def body(i, acc):
        return acc + piece(i * chunk)

    init = jnp.zeros((own_x.shape[0], all_v.shape[1]), jnp.float32)
    return lax.fori_loop(0, steps, body, init)


def split_bf16(values):
    hi = lax.reduce_precision(values, exponent_bits=8, mantissa_bits=7)
    lo = values - hi
    return hi.astype(jnp.bfloat16), lo.astype(jnp.bfloat16)


PERMUTE_GROUP_MAX = 16


def is_power_of_two(n):
    return n & (n - 1) == 0


RING_AXES = ("rows",)


def uses_ring(axis):
    return axis in RING_AXES or not is_power_of_two(lax.axis_size(axis))


def axis_gather(value, axis):
    n = lax.axis_size(axis)
    if uses_ring(axis):
        moved = [value]
        for k in range(1, n):
            perm = [(i, (i + k) % n) for i in range(n)]
            moved.append(lax.ppermute(value, axis, perm))
        return [jnp.concatenate(moved, axis=0)]
    parts = [value]
    bit = n // 2
    while bit >= 1:
        perm = [(i, i ^ bit) for i in range(n)]
        held = parts[0] if len(parts) == 1 else jnp.concatenate(parts, axis=0)
        parts.append(lax.ppermute(held, axis, perm))
        bit //= 2
    return parts


def axis_piece(axis, owner):
    n = lax.axis_size(axis)
    me = lax.axis_index(axis)
    if uses_ring(axis):
        return (me - owner) % n
    d = me ^ owner
    steps = n.bit_length() - 1
    piece = jnp.zeros_like(d)
    for j in range(steps):
        piece = piece + (((d >> (steps - 1 - j)) & 1) << j)
    return piece


def gather_blocks(block):
    n = lax.axis_size("rows") * lax.axis_size("cols")
    if n > PERMUTE_GROUP_MAX:
        got = lax.all_gather(block, ("rows", "cols"), axis=0, tiled=False)
        order = relative_order(jnp.arange(n, dtype=jnp.int32))
        return [jnp.take(got, jnp.argsort(order), axis=0).reshape(-1, block.shape[1])]
    if not uses_ring("rows") or uses_ring("cols"):
        return axis_gather(jnp.concatenate(axis_gather(block, "rows"), axis=0), "cols")
    n_rows = lax.axis_size("rows")
    ring = [lax.ppermute(block, "rows", [(i, (i + k) % n_rows) for i in range(n_rows)]) for k in range(1, n_rows)]
    return pipelined_xor_gather([block, jnp.concatenate(ring, axis=0)], "cols")


def pipelined_xor_gather(parts, axis):
    n = lax.axis_size(axis)
    bit = n // 2
    while bit >= 1:
        perm = [(i, i ^ bit) for i in range(n)]
        if len(parts) == 1:
            parts = parts + [lax.ppermute(parts[0], axis, perm)]
        else:
            held = lax.ppermute(jnp.concatenate(parts[:-1], axis=0), axis, perm)
            newest = lax.ppermute(parts[-1], axis, perm)
            parts = parts + [held, newest]
        bit //= 2
    return parts


def relative_order(owner):
    n_rows = lax.axis_size("rows")
    n_cols = lax.axis_size("cols")
    return axis_piece("cols", owner % n_cols) * n_rows + axis_piece("rows", owner // n_cols)


def projected_all(all_x, all_sq, centers, centers_sq, residual_parts, gamma):
    total = all_x.shape[0]
    chunk = min(COLUMN_CHUNK, total)
    if total % chunk != 0:
        chunk = total
    steps = total // chunk
    contract = (((0,), (0,)), ((), ()))

    if steps == 1:
        c = lax.optimization_barrier(rbf_tile(all_x, all_sq, centers, centers_sq, gamma))
        total_p = None
        begin = 0
        for r in residual_parts:
            piece = lax.slice_in_dim(c, begin, begin + r.shape[0], axis=0)
            term = lax.dot_general(piece, r, contract, preferred_element_type=jnp.float32)
            total_p = term if total_p is None else total_p + term
            begin += r.shape[0]
        return total_p

    residual_b_all = jnp.concatenate(residual_parts, axis=0)

    def piece(start):
        x = lax.dynamic_slice_in_dim(all_x, start, chunk, 0)
        s = lax.dynamic_slice_in_dim(all_sq, start, chunk, 0)
        r = lax.dynamic_slice_in_dim(residual_b_all, start, chunk, 0)
        c = rbf_tile(x, s, centers, centers_sq, gamma)
        return lax.dot_general(c, r, contract, preferred_element_type=jnp.float32)

    def body(i, acc):
        return acc + piece(i * chunk)

    init = jnp.zeros((centers.shape[0], residual_b_all.shape[1]), jnp.float32)
    return lax.fori_loop(0, steps, body, init)


def local(points, solution, targets, inducing, woodbury_inverse):
    gamma = 2.5 / F
    n_local = points.shape[0]
    solution_b = solution.astype(jnp.bfloat16)
    packed = jnp.concatenate([points, solution_b], axis=1)
    parts = gather_blocks(packed)
    own_sq = square_norms(points)
    kp = None
    for part in parts:
        part_x = part[:, :F]
        term = kernel_product(points, own_sq, part_x, square_norms(part_x), part[:, F:], gamma)
        kp = term if kp is None else kp + term
    residual = targets - kp - noise_level * solution
    all_x = jnp.concatenate([part[:, :F] for part in parts], axis=0)
    all_sq = square_norms(all_x)
    owner = inducing // n_local
    position = relative_order(owner) * n_local + inducing % n_local
    centers = jnp.take(all_x, position, axis=0)
    centers_sq = square_norms(centers)
    cross = rbf_tile(points, own_sq, centers, centers_sq, gamma)
    residual_b = residual.astype(jnp.bfloat16)
    res_local = jnp.sum(residual * residual, axis=0)
    tar_local = jnp.sum(targets * targets, axis=0)
    hi, lo = split_bf16(jnp.stack([res_local, tar_local]))
    extra = jnp.zeros((16, residual_b.shape[1]), jnp.bfloat16).at[0:2].set(hi).at[2:4].set(lo)
    sent = jnp.concatenate([residual_b, extra], axis=0)
    width = sent.shape[1]
    gathered_sent = gather_blocks(sent)
    got_parts = [g.reshape(-1, sent.shape[0], width) for g in gathered_sent]
    norms = sum(
        jnp.sum(g[:, n_local:n_local + 2].astype(jnp.float32) + g[:, n_local + 2:n_local + 4].astype(jnp.float32), axis=0)
        for g in got_parts
    )
    res_sq = norms[0]
    tar_sq = norms[1]
    residual_parts = [g[:, :n_local].reshape(-1, width) for g in got_parts]
    projected = projected_all(all_x, all_sq, centers, centers_sq, residual_parts, gamma)
    w_hi, w_lo = split_bf16(woodbury_inverse)
    p_hi, p_lo = split_bf16(projected)
    weights = (
        jnp.dot(w_hi, p_hi, preferred_element_type=jnp.float32)
        + jnp.dot(w_hi, p_lo, preferred_element_type=jnp.float32)
        + jnp.dot(w_lo, p_hi, preferred_element_type=jnp.float32)
    )
    correction = jnp.dot(cross, weights.astype(jnp.bfloat16), preferred_element_type=jnp.float32)
    new_solution = solution + (residual - correction) / noise_level
    relative_norm = jnp.sqrt(res_sq / (tar_sq + 1e-06))
    return (new_solution, residual, relative_norm)


def solution(mesh):
    return jax.shard_map(
        local,
        mesh=mesh,
        in_specs=(
            P(("groups", "rows", "cols"), None),
            P(("groups", "rows", "cols"), None),
            P(("groups", "rows", "cols"), None),
            P("groups"),
            P("groups", None),
        ),
        out_specs=(
            P(("groups", "rows", "cols"), None),
            P(("groups", "rows", "cols"), None),
            P("groups"),
        ),
        check_vma=False,
    )
```

```python
import jax
import jax.numpy as jnp
from jax import lax
from jax.sharding import PartitionSpec as P

F = 128


noise_level = 0.5

COLUMN_CHUNK = 3072


def square_norms(values):
    return jnp.sum(jnp.square(values.astype(jnp.float32)), axis=1)


def rbf_tile(left_x, left_sq, right_x, right_sq, gamma):
    inner = lax.dot_general(
        left_x, right_x, (((1,), (1,)), ((), ())), preferred_element_type=jnp.float32
    )
    return jnp.exp(-gamma * (left_sq[:, None] + right_sq[None, :] - 2.0 * inner)).astype(
        jnp.bfloat16
    )


def kernel_product(own_x, own_sq, all_x, all_sq, all_v, gamma):
    total = all_x.shape[0]
    chunk = min(COLUMN_CHUNK, total)
    if total % chunk != 0:
        chunk = total
    steps = total // chunk

    def piece(start):
        x = lax.dynamic_slice_in_dim(all_x, start, chunk, 0)
        s = lax.dynamic_slice_in_dim(all_sq, start, chunk, 0)
        v = lax.dynamic_slice_in_dim(all_v, start, chunk, 0)
        k = rbf_tile(own_x, own_sq, x, s, gamma)
        return jnp.dot(k, v, preferred_element_type=jnp.float32)

    if steps == 1:
        return piece(0)

    def body(i, acc):
        return acc + piece(i * chunk)

    init = jnp.zeros((own_x.shape[0], all_v.shape[1]), jnp.float32)
    return lax.fori_loop(0, steps, body, init)


def split_bf16(values):
    hi = lax.reduce_precision(values, exponent_bits=8, mantissa_bits=7)
    lo = values - hi
    return hi.astype(jnp.bfloat16), lo.astype(jnp.bfloat16)


PERMUTE_GROUP_MAX = 16


def is_power_of_two(n):
    return n & (n - 1) == 0


RING_AXES = ("rows",)


def uses_ring(axis):
    return axis in RING_AXES or not is_power_of_two(lax.axis_size(axis))


def axis_gather(value, axis):
    n = lax.axis_size(axis)
    if uses_ring(axis):
        moved = [value]
        for k in range(1, n):
            perm = [(i, (i + k) % n) for i in range(n)]
            moved.append(lax.ppermute(value, axis, perm))
        return [jnp.concatenate(moved, axis=0)]
    parts = [value]
    bit = n // 2
    while bit >= 1:
        perm = [(i, i ^ bit) for i in range(n)]
        held = parts[0] if len(parts) == 1 else jnp.concatenate(parts, axis=0)
        parts.append(lax.ppermute(held, axis, perm))
        bit //= 2
    return parts


def axis_piece(axis, owner):
    n = lax.axis_size(axis)
    me = lax.axis_index(axis)
    if uses_ring(axis):
        return (me - owner) % n
    d = me ^ owner
    steps = n.bit_length() - 1
    piece = jnp.zeros_like(d)
    for j in range(steps):
        piece = piece + (((d >> (steps - 1 - j)) & 1) << j)
    return piece


def gather_blocks(block):
    n = lax.axis_size("rows") * lax.axis_size("cols")
    if n > PERMUTE_GROUP_MAX:
        got = lax.all_gather(block, ("rows", "cols"), axis=0, tiled=False)
        order = relative_order(jnp.arange(n, dtype=jnp.int32))
        return [jnp.take(got, jnp.argsort(order), axis=0).reshape(-1, block.shape[1])]
    if not uses_ring("rows") or uses_ring("cols"):
        return axis_gather(jnp.concatenate(axis_gather(block, "rows"), axis=0), "cols")
    n_rows = lax.axis_size("rows")
    ring = [lax.ppermute(block, "rows", [(i, (i + k) % n_rows) for i in range(n_rows)]) for k in range(1, n_rows)]
    return pipelined_xor_gather([block, jnp.concatenate(ring, axis=0)], "cols")


def pipelined_xor_gather(parts, axis):
    n = lax.axis_size(axis)
    bit = n // 2
    while bit >= 1:
        perm = [(i, i ^ bit) for i in range(n)]
        if len(parts) == 1:
            parts = parts + [lax.ppermute(parts[0], axis, perm)]
        else:
            held = lax.ppermute(jnp.concatenate(parts[:-1], axis=0), axis, perm)
            newest = lax.ppermute(parts[-1], axis, perm)
            parts = parts + [held, newest]
        bit //= 2
    return parts


def relative_order(owner):
    n_rows = lax.axis_size("rows")
    n_cols = lax.axis_size("cols")
    return axis_piece("cols", owner % n_cols) * n_rows + axis_piece("rows", owner // n_cols)


def projected_all(all_x, all_sq, centers, centers_sq, residual_parts, gamma):
    total = all_x.shape[0]
    chunk = min(COLUMN_CHUNK, total)
    if total % chunk != 0:
        chunk = total
    steps = total // chunk
    contract = (((0,), (0,)), ((), ()))

    if steps == 1:
        c = lax.optimization_barrier(rbf_tile(all_x, all_sq, centers, centers_sq, gamma))
        total_p = None
        begin = 0
        for r in residual_parts:
            piece = lax.slice_in_dim(c, begin, begin + r.shape[0], axis=0)
            term = lax.dot_general(piece, r, contract, preferred_element_type=jnp.float32)
            total_p = term if total_p is None else total_p + term
            begin += r.shape[0]
        return total_p

    residual_b_all = jnp.concatenate(residual_parts, axis=0)

    def piece(start):
        x = lax.dynamic_slice_in_dim(all_x, start, chunk, 0)
        s = lax.dynamic_slice_in_dim(all_sq, start, chunk, 0)
        r = lax.dynamic_slice_in_dim(residual_b_all, start, chunk, 0)
        c = rbf_tile(x, s, centers, centers_sq, gamma)
        return lax.dot_general(c, r, contract, preferred_element_type=jnp.float32)

    def body(i, acc):
        return acc + piece(i * chunk)

    init = jnp.zeros((centers.shape[0], residual_b_all.shape[1]), jnp.float32)
    return lax.fori_loop(0, steps, body, init)


def local(points, solution, targets, inducing, woodbury_inverse):
    gamma = 2.5 / F
    n_local = points.shape[0]
    solution_b = solution.astype(jnp.bfloat16)
    packed = jnp.concatenate([points, solution_b], axis=1)
    parts = gather_blocks(packed)
    own_sq = square_norms(points)
    kp = None
    for part in parts:
        part_x = part[:, :F]
        term = kernel_product(points, own_sq, part_x, square_norms(part_x), part[:, F:], gamma)
        kp = term if kp is None else kp + term
    residual = targets - kp - noise_level * solution
    all_x = jnp.concatenate([part[:, :F] for part in parts], axis=0)
    all_sq = square_norms(all_x)
    owner = inducing // n_local
    position = relative_order(owner) * n_local + inducing % n_local
    selector = (position[:, None] == jnp.arange(all_x.shape[0], dtype=position.dtype)[None, :]).astype(
        jnp.bfloat16
    )
    centers = jnp.dot(selector, all_x, preferred_element_type=jnp.float32).astype(jnp.bfloat16)
    centers_sq = square_norms(centers)
    cross = rbf_tile(points, own_sq, centers, centers_sq, gamma)
    residual_b = residual.astype(jnp.bfloat16)
    res_local = jnp.sum(residual * residual, axis=0)
    tar_local = jnp.sum(targets * targets, axis=0)
    hi, lo = split_bf16(jnp.stack([res_local, tar_local]))
    extra = jnp.zeros((16, residual_b.shape[1]), jnp.bfloat16).at[0:2].set(hi).at[2:4].set(lo)
    sent = jnp.concatenate([residual_b, extra], axis=0)
    width = sent.shape[1]
    gathered_sent = gather_blocks(sent)
    got_parts = [g.reshape(-1, sent.shape[0], width) for g in gathered_sent]
    norms = sum(
        jnp.sum(g[:, n_local:n_local + 2].astype(jnp.float32) + g[:, n_local + 2:n_local + 4].astype(jnp.float32), axis=0)
        for g in got_parts
    )
    res_sq = norms[0]
    tar_sq = norms[1]
    residual_parts = [g[:, :n_local].reshape(-1, width) for g in got_parts]
    projected = projected_all(all_x, all_sq, centers, centers_sq, residual_parts, gamma)
    w_hi, w_lo = split_bf16(woodbury_inverse)
    p_hi, p_lo = split_bf16(projected)
    weights = (
        jnp.dot(w_hi, p_hi, preferred_element_type=jnp.float32)
        + jnp.dot(w_hi, p_lo, preferred_element_type=jnp.float32)
        + jnp.dot(w_lo, p_hi, preferred_element_type=jnp.float32)
    )
    correction = jnp.dot(cross, weights.astype(jnp.bfloat16), preferred_element_type=jnp.float32)
    new_solution = solution + (residual - correction) / noise_level
    relative_norm = jnp.sqrt(res_sq / (tar_sq + 1e-06))
    return (new_solution, residual, relative_norm)


def solution(mesh):
    return jax.shard_map(
        local,
        mesh=mesh,
        in_specs=(
            P(("groups", "rows", "cols"), None),
            P(("groups", "rows", "cols"), None),
            P(("groups", "rows", "cols"), None),
            P("groups"),
            P("groups", None),
        ),
        out_specs=(
            P(("groups", "rows", "cols"), None),
            P(("groups", "rows", "cols"), None),
            P("groups"),
        ),
        check_vma=False,
    )
```

```python
import jax
import jax.numpy as jnp
from jax import lax
from jax.sharding import PartitionSpec as P

F = 128


noise_level = 0.5

COLUMN_CHUNK = 3072


def square_norms(values):
    return jnp.sum(jnp.square(values.astype(jnp.float32)), axis=1)


def rbf_tile(left_x, left_sq, right_x, right_sq, gamma):
    inner = lax.dot_general(
        left_x, right_x, (((1,), (1,)), ((), ())), preferred_element_type=jnp.float32
    )
    return jnp.exp(-gamma * (left_sq[:, None] + right_sq[None, :] - 2.0 * inner)).astype(
        jnp.bfloat16
    )


def kernel_product(own_x, own_sq, all_x, all_sq, all_v, gamma):
    total = all_x.shape[0]
    chunk = min(COLUMN_CHUNK, total)
    if total % chunk != 0:
        chunk = total
    steps = total // chunk

    def piece(start):
        x = lax.dynamic_slice_in_dim(all_x, start, chunk, 0)
        s = lax.dynamic_slice_in_dim(all_sq, start, chunk, 0)
        v = lax.dynamic_slice_in_dim(all_v, start, chunk, 0)
        k = rbf_tile(own_x, own_sq, x, s, gamma)
        return jnp.dot(k, v, preferred_element_type=jnp.float32)

    if steps == 1:
        return piece(0)

    def body(i, acc):
        return acc + piece(i * chunk)

    init = jnp.zeros((own_x.shape[0], all_v.shape[1]), jnp.float32)
    return lax.fori_loop(0, steps, body, init)


def split_bf16(values):
    hi = lax.reduce_precision(values, exponent_bits=8, mantissa_bits=7)
    lo = values - hi
    return hi.astype(jnp.bfloat16), lo.astype(jnp.bfloat16)


PERMUTE_GROUP_MAX = 16


def is_power_of_two(n):
    return n & (n - 1) == 0


RING_AXES = ("rows",)


def uses_ring(axis):
    return axis in RING_AXES or not is_power_of_two(lax.axis_size(axis))


def axis_gather(value, axis):
    n = lax.axis_size(axis)
    if uses_ring(axis):
        moved = [value]
        for k in range(1, n):
            perm = [(i, (i + k) % n) for i in range(n)]
            moved.append(lax.ppermute(value, axis, perm))
        return [jnp.concatenate(moved, axis=0)]
    parts = [value]
    bit = n // 2
    while bit >= 1:
        perm = [(i, i ^ bit) for i in range(n)]
        held = parts[0] if len(parts) == 1 else jnp.concatenate(parts, axis=0)
        parts.append(lax.ppermute(held, axis, perm))
        bit //= 2
    return parts


def axis_piece(axis, owner):
    n = lax.axis_size(axis)
    me = lax.axis_index(axis)
    if uses_ring(axis):
        return (me - owner) % n
    d = me ^ owner
    steps = n.bit_length() - 1
    piece = jnp.zeros_like(d)
    for j in range(steps):
        piece = piece + (((d >> (steps - 1 - j)) & 1) << j)
    return piece


def gather_blocks(block, split_pieces=False):
    n = lax.axis_size("rows") * lax.axis_size("cols")
    if n > PERMUTE_GROUP_MAX:
        got = lax.all_gather(block, ("rows", "cols"), axis=0, tiled=False)
        order = relative_order(jnp.arange(n, dtype=jnp.int32))
        return [jnp.take(got, jnp.argsort(order), axis=0).reshape(-1, block.shape[1])]
    if not uses_ring("rows") or uses_ring("cols"):
        return axis_gather(jnp.concatenate(axis_gather(block, "rows"), axis=0), "cols")
    n_rows = lax.axis_size("rows")
    ring = [lax.ppermute(block, "rows", [(i, (i + k) % n_rows) for i in range(n_rows)]) for k in range(1, n_rows)]
    if split_pieces:
        return pipelined_xor_gather([block] + ring, "cols", split_first=True)
    return pipelined_xor_gather([block, jnp.concatenate(ring, axis=0)], "cols")


def pipelined_xor_gather(parts, axis, split_first=False):
    n = lax.axis_size(axis)
    bit = n // 2
    while bit >= 1:
        perm = [(i, i ^ bit) for i in range(n)]
        if len(parts) == 1 or (split_first and bit == n // 2):
            parts = parts + [lax.ppermute(p, axis, perm) for p in parts]
        else:
            held = lax.ppermute(jnp.concatenate(parts[:-1], axis=0), axis, perm)
            newest = lax.ppermute(parts[-1], axis, perm)
            parts = parts + [held, newest]
        bit //= 2
    return parts


def relative_order(owner):
    n_rows = lax.axis_size("rows")
    n_cols = lax.axis_size("cols")
    return axis_piece("cols", owner % n_cols) * n_rows + axis_piece("rows", owner // n_cols)


def projected_all(all_x, all_sq, centers, centers_sq, residual_parts, gamma):
    total = all_x.shape[0]
    chunk = min(COLUMN_CHUNK, total)
    if total % chunk != 0:
        chunk = total
    steps = total // chunk
    contract = (((0,), (0,)), ((), ()))

    if steps == 1:
        c = lax.optimization_barrier(rbf_tile(all_x, all_sq, centers, centers_sq, gamma))
        total_p = None
        begin = 0
        for r in residual_parts:
            piece = lax.slice_in_dim(c, begin, begin + r.shape[0], axis=0)
            term = lax.dot_general(piece, r, contract, preferred_element_type=jnp.float32)
            total_p = term if total_p is None else total_p + term
            begin += r.shape[0]
        return total_p

    residual_b_all = jnp.concatenate(residual_parts, axis=0)

    def piece(start):
        x = lax.dynamic_slice_in_dim(all_x, start, chunk, 0)
        s = lax.dynamic_slice_in_dim(all_sq, start, chunk, 0)
        r = lax.dynamic_slice_in_dim(residual_b_all, start, chunk, 0)
        c = rbf_tile(x, s, centers, centers_sq, gamma)
        return lax.dot_general(c, r, contract, preferred_element_type=jnp.float32)

    def body(i, acc):
        return acc + piece(i * chunk)

    init = jnp.zeros((centers.shape[0], residual_b_all.shape[1]), jnp.float32)
    return lax.fori_loop(0, steps, body, init)


def local(points, solution, targets, inducing, woodbury_inverse):
    gamma = 2.5 / F
    n_local = points.shape[0]
    solution_b = solution.astype(jnp.bfloat16)
    packed = jnp.concatenate([points, solution_b], axis=1)
    parts = gather_blocks(packed, split_pieces=True)
    own_sq = square_norms(points)
    kp = None
    for part in parts:
        part_x = part[:, :F]
        term = kernel_product(points, own_sq, part_x, square_norms(part_x), part[:, F:], gamma)
        kp = term if kp is None else kp + term
    residual = targets - kp - noise_level * solution
    all_x = jnp.concatenate([part[:, :F] for part in parts], axis=0)
    all_sq = square_norms(all_x)
    owner = inducing // n_local
    position = relative_order(owner) * n_local + inducing % n_local
    centers = jnp.take(all_x, position, axis=0)
    centers_sq = square_norms(centers)
    cross = rbf_tile(points, own_sq, centers, centers_sq, gamma)
    residual_b = residual.astype(jnp.bfloat16)
    res_local = jnp.sum(residual * residual, axis=0)
    tar_local = jnp.sum(targets * targets, axis=0)
    hi, lo = split_bf16(jnp.stack([res_local, tar_local]))
    extra = jnp.zeros((16, residual_b.shape[1]), jnp.bfloat16).at[0:2].set(hi).at[2:4].set(lo)
    sent = jnp.concatenate([residual_b, extra], axis=0)
    width = sent.shape[1]
    gathered_sent = gather_blocks(sent)
    got_parts = [g.reshape(-1, sent.shape[0], width) for g in gathered_sent]
    norms = sum(
        jnp.sum(g[:, n_local:n_local + 2].astype(jnp.float32) + g[:, n_local + 2:n_local + 4].astype(jnp.float32), axis=0)
        for g in got_parts
    )
    res_sq = norms[0]
    tar_sq = norms[1]
    residual_parts = [g[:, :n_local].reshape(-1, width) for g in got_parts]
    projected = projected_all(all_x, all_sq, centers, centers_sq, residual_parts, gamma)
    w_hi, w_lo = split_bf16(woodbury_inverse)
    p_hi, p_lo = split_bf16(projected)
    weights = (
        jnp.dot(w_hi, p_hi, preferred_element_type=jnp.float32)
        + jnp.dot(w_hi, p_lo, preferred_element_type=jnp.float32)
        + jnp.dot(w_lo, p_hi, preferred_element_type=jnp.float32)
    )
    correction = jnp.dot(cross, weights.astype(jnp.bfloat16), preferred_element_type=jnp.float32)
    new_solution = solution + (residual - correction) / noise_level
    relative_norm = jnp.sqrt(res_sq / (tar_sq + 1e-06))
    return (new_solution, residual, relative_norm)


def solution(mesh):
    return jax.shard_map(
        local,
        mesh=mesh,
        in_specs=(
            P(("groups", "rows", "cols"), None),
            P(("groups", "rows", "cols"), None),
            P(("groups", "rows", "cols"), None),
            P("groups"),
            P("groups", None),
        ),
        out_specs=(
            P(("groups", "rows", "cols"), None),
            P(("groups", "rows", "cols"), None),
            P("groups"),
        ),
        check_vma=False,
    )
```

```python
import jax
import jax.numpy as jnp
from jax import lax
from jax.sharding import PartitionSpec as P

F = 128


noise_level = 0.5

COLUMN_CHUNK = 3072


def square_norms(values):
    return jnp.sum(jnp.square(values.astype(jnp.float32)), axis=1)


def rbf_tile(left_x, left_sq, right_x, right_sq, gamma):
    inner = lax.dot_general(
        left_x, right_x, (((1,), (1,)), ((), ())), preferred_element_type=jnp.float32
    )
    return jnp.exp(-gamma * (left_sq[:, None] + right_sq[None, :] - 2.0 * inner)).astype(
        jnp.bfloat16
    )


def kernel_product(own_x, own_sq, all_x, all_sq, all_v, gamma):
    total = all_x.shape[0]
    chunk = min(COLUMN_CHUNK, total)
    if total % chunk != 0:
        chunk = total
    steps = total // chunk

    def piece(start):
        x = lax.dynamic_slice_in_dim(all_x, start, chunk, 0)
        s = lax.dynamic_slice_in_dim(all_sq, start, chunk, 0)
        v = lax.dynamic_slice_in_dim(all_v, start, chunk, 0)
        k = rbf_tile(own_x, own_sq, x, s, gamma)
        return jnp.dot(k, v, preferred_element_type=jnp.float32)

    if steps == 1:
        return piece(0)

    def body(i, acc):
        return acc + piece(i * chunk)

    init = jnp.zeros((own_x.shape[0], all_v.shape[1]), jnp.float32)
    return lax.fori_loop(0, steps, body, init)


def split_bf16(values):
    hi = lax.reduce_precision(values, exponent_bits=8, mantissa_bits=7)
    lo = values - hi
    return hi.astype(jnp.bfloat16), lo.astype(jnp.bfloat16)


PERMUTE_GROUP_MAX = 16


def is_power_of_two(n):
    return n & (n - 1) == 0


RING_AXES = ("rows",)


def uses_ring(axis):
    return axis in RING_AXES or not is_power_of_two(lax.axis_size(axis))


def axis_gather(value, axis):
    n = lax.axis_size(axis)
    if uses_ring(axis):
        moved = [value]
        for k in range(1, n):
            perm = [(i, (i + k) % n) for i in range(n)]
            moved.append(lax.ppermute(value, axis, perm))
        return [jnp.concatenate(moved, axis=0)]
    parts = [value]
    bit = n // 2
    while bit >= 1:
        perm = [(i, i ^ bit) for i in range(n)]
        held = parts[0] if len(parts) == 1 else jnp.concatenate(parts, axis=0)
        parts.append(lax.ppermute(held, axis, perm))
        bit //= 2
    return parts


def axis_piece(axis, owner):
    n = lax.axis_size(axis)
    me = lax.axis_index(axis)
    if uses_ring(axis):
        return (me - owner) % n
    d = me ^ owner
    steps = n.bit_length() - 1
    piece = jnp.zeros_like(d)
    for j in range(steps):
        piece = piece + (((d >> (steps - 1 - j)) & 1) << j)
    return piece


def gather_blocks(block, split_pieces=False):
    n = lax.axis_size("rows") * lax.axis_size("cols")
    if n > PERMUTE_GROUP_MAX:
        got = lax.all_gather(block, ("rows", "cols"), axis=0, tiled=False)
        order = relative_order(jnp.arange(n, dtype=jnp.int32))
        return [jnp.take(got, jnp.argsort(order), axis=0).reshape(-1, block.shape[1])]
    if not uses_ring("rows") or uses_ring("cols"):
        return axis_gather(jnp.concatenate(axis_gather(block, "rows"), axis=0), "cols")
    n_rows = lax.axis_size("rows")
    ring = [lax.ppermute(block, "rows", [(i, (i + k) % n_rows) for i in range(n_rows)]) for k in range(1, n_rows)]
    if split_pieces:
        return pipelined_xor_gather([block] + ring, "cols", split_first=True)
    return pipelined_xor_gather([block, jnp.concatenate(ring, axis=0)], "cols")


def pipelined_xor_gather(parts, axis, split_first=False):
    n = lax.axis_size(axis)
    bit = n // 2
    while bit >= 1:
        perm = [(i, i ^ bit) for i in range(n)]
        if len(parts) == 1 or (split_first and bit == n // 2):
            parts = parts + [lax.ppermute(p, axis, perm) for p in parts]
        else:
            held = lax.ppermute(jnp.concatenate(parts[:-1], axis=0), axis, perm)
            newest = lax.ppermute(parts[-1], axis, perm)
            parts = parts + [held, newest]
        bit //= 2
    return parts


def relative_order(owner):
    n_rows = lax.axis_size("rows")
    n_cols = lax.axis_size("cols")
    return axis_piece("cols", owner % n_cols) * n_rows + axis_piece("rows", owner // n_cols)


def projected_all(all_x, all_sq, centers, centers_sq, residual_parts, gamma):
    total = all_x.shape[0]
    chunk = min(COLUMN_CHUNK, total)
    if total % chunk != 0:
        chunk = total
    steps = total // chunk
    contract = (((0,), (0,)), ((), ()))

    if steps == 1:
        c = lax.optimization_barrier(rbf_tile(all_x, all_sq, centers, centers_sq, gamma))
        total_p = None
        begin = 0
        for r in residual_parts:
            piece = lax.slice_in_dim(c, begin, begin + r.shape[0], axis=0)
            term = lax.dot_general(piece, r, contract, preferred_element_type=jnp.float32)
            total_p = term if total_p is None else total_p + term
            begin += r.shape[0]
        return total_p, c

    residual_b_all = jnp.concatenate(residual_parts, axis=0)

    def piece(start):
        x = lax.dynamic_slice_in_dim(all_x, start, chunk, 0)
        s = lax.dynamic_slice_in_dim(all_sq, start, chunk, 0)
        r = lax.dynamic_slice_in_dim(residual_b_all, start, chunk, 0)
        c = rbf_tile(x, s, centers, centers_sq, gamma)
        return lax.dot_general(c, r, contract, preferred_element_type=jnp.float32)

    def body(i, acc):
        return acc + piece(i * chunk)

    init = jnp.zeros((centers.shape[0], residual_b_all.shape[1]), jnp.float32)
    return lax.fori_loop(0, steps, body, init), None


def local(points, solution, targets, inducing, woodbury_inverse):
    gamma = 2.5 / F
    n_local = points.shape[0]
    solution_b = solution.astype(jnp.bfloat16)
    packed = jnp.concatenate([points, solution_b], axis=1)
    parts = gather_blocks(packed, split_pieces=True)
    own_sq = square_norms(points)
    kp = None
    for part in parts:
        part_x = part[:, :F]
        term = kernel_product(points, own_sq, part_x, square_norms(part_x), part[:, F:], gamma)
        kp = term if kp is None else kp + term
    residual = targets - kp - noise_level * solution
    all_x = jnp.concatenate([part[:, :F] for part in parts], axis=0)
    all_sq = square_norms(all_x)
    owner = inducing // n_local
    position = relative_order(owner) * n_local + inducing % n_local
    centers = jnp.take(all_x, position, axis=0)
    centers_sq = square_norms(centers)
    cross = rbf_tile(points, own_sq, centers, centers_sq, gamma)
    residual_b = residual.astype(jnp.bfloat16)
    res_local = jnp.sum(residual * residual, axis=0)
    tar_local = jnp.sum(targets * targets, axis=0)
    hi, lo = split_bf16(jnp.stack([res_local, tar_local]))
    extra = jnp.zeros((16, residual_b.shape[1]), jnp.bfloat16).at[0:2].set(hi).at[2:4].set(lo)
    sent = jnp.concatenate([residual_b, extra], axis=0)
    width = sent.shape[1]
    gathered_sent = gather_blocks(sent)
    got_parts = [g.reshape(-1, sent.shape[0], width) for g in gathered_sent]
    norms = sum(
        jnp.sum(g[:, n_local:n_local + 2].astype(jnp.float32) + g[:, n_local + 2:n_local + 4].astype(jnp.float32), axis=0)
        for g in got_parts
    )
    res_sq = norms[0]
    tar_sq = norms[1]
    residual_parts = [g[:, :n_local].reshape(-1, width) for g in got_parts]
    projected, cross_all = projected_all(all_x, all_sq, centers, centers_sq, residual_parts, gamma)
    if cross_all is not None:
        cross = lax.slice_in_dim(cross_all, 0, n_local, axis=0)
    w_hi, w_lo = split_bf16(woodbury_inverse)
    p_hi, p_lo = split_bf16(projected)
    weights = (
        jnp.dot(w_hi, p_hi, preferred_element_type=jnp.float32)
        + jnp.dot(w_hi, p_lo, preferred_element_type=jnp.float32)
        + jnp.dot(w_lo, p_hi, preferred_element_type=jnp.float32)
    )
    correction = jnp.dot(cross, weights.astype(jnp.bfloat16), preferred_element_type=jnp.float32)
    new_solution = solution + (residual - correction) / noise_level
    relative_norm = jnp.sqrt(res_sq / (tar_sq + 1e-06))
    return (new_solution, residual, relative_norm)


def solution(mesh):
    return jax.shard_map(
        local,
        mesh=mesh,
        in_specs=(
            P(("groups", "rows", "cols"), None),
            P(("groups", "rows", "cols"), None),
            P(("groups", "rows", "cols"), None),
            P("groups"),
            P("groups", None),
        ),
        out_specs=(
            P(("groups", "rows", "cols"), None),
            P(("groups", "rows", "cols"), None),
            P("groups"),
        ),
        check_vma=False,
    )
```

```python
import jax
import jax.numpy as jnp
from jax import lax
from jax.sharding import PartitionSpec as P

F = 128


noise_level = 0.5

COLUMN_CHUNK = 3072


def square_norms(values):
    return jnp.sum(jnp.square(values.astype(jnp.float32)), axis=1)


def rbf_tile(left_x, left_sq, right_x, right_sq, gamma):
    inner = lax.dot_general(
        left_x, right_x, (((1,), (1,)), ((), ())), preferred_element_type=jnp.float32
    )
    return jnp.exp(-gamma * (left_sq[:, None] + right_sq[None, :] - 2.0 * inner)).astype(
        jnp.bfloat16
    )


def kernel_product(own_x, own_sq, all_x, all_sq, all_v, gamma):
    total = all_x.shape[0]
    chunk = min(COLUMN_CHUNK, total)
    if total % chunk != 0:
        chunk = total
    steps = total // chunk

    def piece(start):
        x = lax.dynamic_slice_in_dim(all_x, start, chunk, 0)
        s = lax.dynamic_slice_in_dim(all_sq, start, chunk, 0)
        v = lax.dynamic_slice_in_dim(all_v, start, chunk, 0)
        k = rbf_tile(own_x, own_sq, x, s, gamma)
        return jnp.dot(k, v, preferred_element_type=jnp.float32)

    if steps == 1:
        return piece(0)

    def body(i, acc):
        return acc + piece(i * chunk)

    init = jnp.zeros((own_x.shape[0], all_v.shape[1]), jnp.float32)
    return lax.fori_loop(0, steps, body, init)


def split_bf16(values):
    hi = lax.reduce_precision(values, exponent_bits=8, mantissa_bits=7)
    lo = values - hi
    return hi.astype(jnp.bfloat16), lo.astype(jnp.bfloat16)


PERMUTE_GROUP_MAX = 16


def is_power_of_two(n):
    return n & (n - 1) == 0


RING_AXES = ("rows",)


def uses_ring(axis):
    return axis in RING_AXES or not is_power_of_two(lax.axis_size(axis))


def axis_gather(value, axis):
    n = lax.axis_size(axis)
    if uses_ring(axis):
        moved = [value]
        for k in range(1, n):
            perm = [(i, (i + k) % n) for i in range(n)]
            moved.append(lax.ppermute(value, axis, perm))
        return [jnp.concatenate(moved, axis=0)]
    parts = [value]
    bit = n // 2
    while bit >= 1:
        perm = [(i, i ^ bit) for i in range(n)]
        held = parts[0] if len(parts) == 1 else jnp.concatenate(parts, axis=0)
        parts.append(lax.ppermute(held, axis, perm))
        bit //= 2
    return parts


def axis_piece(axis, owner):
    n = lax.axis_size(axis)
    me = lax.axis_index(axis)
    if uses_ring(axis):
        return (me - owner) % n
    d = me ^ owner
    steps = n.bit_length() - 1
    piece = jnp.zeros_like(d)
    for j in range(steps):
        piece = piece + (((d >> (steps - 1 - j)) & 1) << j)
    return piece


def gather_blocks(block, split_pieces=False):
    n = lax.axis_size("rows") * lax.axis_size("cols")
    if n > PERMUTE_GROUP_MAX:
        got = lax.all_gather(block, ("rows", "cols"), axis=0, tiled=False)
        order = relative_order(jnp.arange(n, dtype=jnp.int32))
        return [jnp.take(got, jnp.argsort(order), axis=0).reshape(-1, block.shape[1])]
    if not uses_ring("rows") or uses_ring("cols"):
        return axis_gather(jnp.concatenate(axis_gather(block, "rows"), axis=0), "cols")
    n_rows = lax.axis_size("rows")
    ring = [lax.ppermute(block, "rows", [(i, (i + k) % n_rows) for i in range(n_rows)]) for k in range(1, n_rows)]
    if split_pieces:
        return pipelined_xor_gather([block] + ring, "cols", split_first=True)
    return pipelined_xor_gather([block, jnp.concatenate(ring, axis=0)], "cols")


def pipelined_xor_gather(parts, axis, split_first=False):
    n = lax.axis_size(axis)
    bit = n // 2
    while bit >= 1:
        perm = [(i, i ^ bit) for i in range(n)]
        if len(parts) == 1 or (split_first and bit == n // 2):
            parts = parts + [lax.ppermute(p, axis, perm) for p in parts]
        else:
            held = lax.ppermute(jnp.concatenate(parts[:-1], axis=0), axis, perm)
            newest = lax.ppermute(parts[-1], axis, perm)
            parts = parts + [held, newest]
        bit //= 2
    return parts


def relative_order(owner):
    n_rows = lax.axis_size("rows")
    n_cols = lax.axis_size("cols")
    return axis_piece("cols", owner % n_cols) * n_rows + axis_piece("rows", owner // n_cols)


def projected_all(all_x, all_sq, centers, centers_sq, residual_parts, gamma):
    total = all_x.shape[0]
    chunk = min(COLUMN_CHUNK, total)
    if total % chunk != 0:
        chunk = total
    steps = total // chunk
    contract = (((0,), (0,)), ((), ()))

    if steps == 1:
        c = lax.optimization_barrier(rbf_tile(all_x, all_sq, centers, centers_sq, gamma))
        total_p = None
        begin = 0
        for r in residual_parts:
            piece = lax.slice_in_dim(c, begin, begin + r.shape[0], axis=0)
            term = lax.dot_general(piece, r, contract, preferred_element_type=jnp.float32)
            total_p = term if total_p is None else total_p + term
            begin += r.shape[0]
        return total_p

    residual_b_all = jnp.concatenate(residual_parts, axis=0)

    def piece(start):
        x = lax.dynamic_slice_in_dim(all_x, start, chunk, 0)
        s = lax.dynamic_slice_in_dim(all_sq, start, chunk, 0)
        r = lax.dynamic_slice_in_dim(residual_b_all, start, chunk, 0)
        c = rbf_tile(x, s, centers, centers_sq, gamma)
        return lax.dot_general(c, r, contract, preferred_element_type=jnp.float32)

    def body(i, acc):
        return acc + piece(i * chunk)

    init = jnp.zeros((centers.shape[0], residual_b_all.shape[1]), jnp.float32)
    return lax.fori_loop(0, steps, body, init)


def local(points, solution, targets, inducing, woodbury_inverse):
    gamma = 2.5 / F
    n_local = points.shape[0]
    solution_b = solution.astype(jnp.bfloat16)
    packed = jnp.concatenate([points, solution_b], axis=1)
    parts = gather_blocks(packed, split_pieces=True)
    own_sq = square_norms(points)
    kp = None
    for part in parts:
        part_x = part[:, :F]
        term = kernel_product(points, own_sq, part_x, square_norms(part_x), part[:, F:], gamma)
        kp = term if kp is None else kp + term
    residual = targets - kp - noise_level * solution
    all_x = jnp.concatenate([part[:, :F] for part in parts], axis=0)
    all_sq = square_norms(all_x)
    owner = inducing // n_local
    position = relative_order(owner) * n_local + inducing % n_local
    centers = jnp.take(all_x, position, axis=0)
    centers_sq = square_norms(centers)
    cross = rbf_tile(points, own_sq, centers, centers_sq, gamma)
    residual_b = residual.astype(jnp.bfloat16)
    res_local = jnp.sum(residual * residual, axis=0)
    tar_local = jnp.sum(targets * targets, axis=0)
    hi, lo = split_bf16(jnp.stack([res_local, tar_local]))
    extra = jnp.zeros((16, residual_b.shape[1]), jnp.bfloat16).at[0:2].set(hi).at[2:4].set(lo)
    sent = jnp.concatenate([residual_b, extra], axis=0)
    width = sent.shape[1]
    gathered_sent = gather_blocks(sent)
    got_parts = [g.reshape(-1, sent.shape[0], width) for g in gathered_sent]
    norms = sum(
        jnp.sum(g[:, n_local:n_local + 2].astype(jnp.float32) + g[:, n_local + 2:n_local + 4].astype(jnp.float32), axis=0)
        for g in got_parts
    )
    res_sq = norms[0]
    tar_sq = norms[1]
    residual_parts = [g[:, :n_local].reshape(-1, width) for g in got_parts]
    projected = projected_all(all_x, all_sq, centers, centers_sq, residual_parts, gamma)
    w_hi, w_lo = split_bf16(woodbury_inverse)
    p_hi, p_lo = split_bf16(projected)
    w_both = jnp.concatenate([w_hi, w_lo], axis=1)
    p_both = jnp.concatenate(
        [jnp.concatenate([p_hi, p_lo], axis=1), jnp.concatenate([p_hi, jnp.zeros_like(p_lo)], axis=1)], axis=0
    )
    both = jnp.dot(w_both, p_both, preferred_element_type=jnp.float32)
    r = p_hi.shape[1]
    weights = both[:, :r] + both[:, r:]
    correction = jnp.dot(cross, weights.astype(jnp.bfloat16), preferred_element_type=jnp.float32)
    new_solution = solution + (residual - correction) / noise_level
    relative_norm = jnp.sqrt(res_sq / (tar_sq + 1e-06))
    return (new_solution, residual, relative_norm)


def solution(mesh):
    return jax.shard_map(
        local,
        mesh=mesh,
        in_specs=(
            P(("groups", "rows", "cols"), None),
            P(("groups", "rows", "cols"), None),
            P(("groups", "rows", "cols"), None),
            P("groups"),
            P("groups", None),
        ),
        out_specs=(
            P(("groups", "rows", "cols"), None),
            P(("groups", "rows", "cols"), None),
            P("groups"),
        ),
        check_vma=False,
    )
```

```python
import jax
import jax.numpy as jnp
from jax import lax
from jax.sharding import PartitionSpec as P

F = 128


noise_level = 0.5

COLUMN_CHUNK = 3072


def square_norms(values):
    return jnp.sum(jnp.square(values.astype(jnp.float32)), axis=1)


def rbf_tile(left_x, left_sq, right_x, right_sq, gamma):
    inner = lax.dot_general(
        left_x, right_x, (((1,), (1,)), ((), ())), preferred_element_type=jnp.float32
    )
    return jnp.exp(-gamma * (left_sq[:, None] + right_sq[None, :] - 2.0 * inner)).astype(
        jnp.bfloat16
    )


def kernel_product(own_x, own_sq, all_x, all_sq, all_v, gamma):
    total = all_x.shape[0]
    chunk = min(COLUMN_CHUNK, total)
    if total % chunk != 0:
        chunk = total
    steps = total // chunk

    def piece(start):
        x = lax.dynamic_slice_in_dim(all_x, start, chunk, 0)
        s = lax.dynamic_slice_in_dim(all_sq, start, chunk, 0)
        v = lax.dynamic_slice_in_dim(all_v, start, chunk, 0)
        k = rbf_tile(own_x, own_sq, x, s, gamma)
        return jnp.dot(k, v, preferred_element_type=jnp.float32)

    if steps == 1:
        return piece(0)

    def body(i, acc):
        return acc + piece(i * chunk)

    init = jnp.zeros((own_x.shape[0], all_v.shape[1]), jnp.float32)
    return lax.fori_loop(0, steps, body, init)


def split_bf16(values):
    hi = lax.reduce_precision(values, exponent_bits=8, mantissa_bits=7)
    lo = values - hi
    return hi.astype(jnp.bfloat16), lo.astype(jnp.bfloat16)


PERMUTE_GROUP_MAX = 16


def is_power_of_two(n):
    return n & (n - 1) == 0


RING_AXES = ("rows",)


def uses_ring(axis):
    return axis in RING_AXES or not is_power_of_two(lax.axis_size(axis))


def axis_gather(value, axis):
    n = lax.axis_size(axis)
    if uses_ring(axis):
        moved = [value]
        for k in range(1, n):
            perm = [(i, (i + k) % n) for i in range(n)]
            moved.append(lax.ppermute(value, axis, perm))
        return [jnp.concatenate(moved, axis=0)]
    parts = [value]
    bit = n // 2
    while bit >= 1:
        perm = [(i, i ^ bit) for i in range(n)]
        held = parts[0] if len(parts) == 1 else jnp.concatenate(parts, axis=0)
        parts.append(lax.ppermute(held, axis, perm))
        bit //= 2
    return parts


def axis_piece(axis, owner):
    n = lax.axis_size(axis)
    me = lax.axis_index(axis)
    if uses_ring(axis):
        return (me - owner) % n
    d = me ^ owner
    steps = n.bit_length() - 1
    piece = jnp.zeros_like(d)
    for j in range(steps):
        piece = piece + (((d >> (steps - 1 - j)) & 1) << j)
    return piece


def gather_blocks(block, split_pieces=False):
    n = lax.axis_size("rows") * lax.axis_size("cols")
    if n > PERMUTE_GROUP_MAX:
        got = lax.all_gather(block, ("rows", "cols"), axis=0, tiled=False)
        order = relative_order(jnp.arange(n, dtype=jnp.int32))
        return [jnp.take(got, jnp.argsort(order), axis=0).reshape(-1, block.shape[1])]
    if not uses_ring("rows") or uses_ring("cols"):
        return axis_gather(jnp.concatenate(axis_gather(block, "rows"), axis=0), "cols")
    n_rows = lax.axis_size("rows")
    ring = [lax.ppermute(block, "rows", [(i, (i + k) % n_rows) for i in range(n_rows)]) for k in range(1, n_rows)]
    if split_pieces:
        return pipelined_xor_gather([block] + ring, "cols", split_first=True)
    return pipelined_xor_gather([block, jnp.concatenate(ring, axis=0)], "cols")


def pipelined_xor_gather(parts, axis, split_first=False):
    n = lax.axis_size(axis)
    bit = n // 2
    while bit >= 1:
        perm = [(i, i ^ bit) for i in range(n)]
        if len(parts) == 1 or (split_first and bit == n // 2):
            parts = parts + [lax.ppermute(p, axis, perm) for p in parts]
        else:
            held = lax.ppermute(jnp.concatenate(parts[:-1], axis=0), axis, perm)
            newest = lax.ppermute(parts[-1], axis, perm)
            parts = parts + [held, newest]
        bit //= 2
    return parts


def relative_order(owner):
    n_rows = lax.axis_size("rows")
    n_cols = lax.axis_size("cols")
    return axis_piece("cols", owner % n_cols) * n_rows + axis_piece("rows", owner // n_cols)


def projected_all(all_x, all_sq, centers, centers_sq, residual_parts, gamma):
    total = all_x.shape[0]
    chunk = min(COLUMN_CHUNK, total)
    if total % chunk != 0:
        chunk = total
    steps = total // chunk
    contract = (((0,), (0,)), ((), ()))

    if steps == 1:
        c = lax.optimization_barrier(rbf_tile(all_x, all_sq, centers, centers_sq, gamma))
        total_p = None
        begin = 0
        for r in residual_parts:
            piece = lax.slice_in_dim(c, begin, begin + r.shape[0], axis=0)
            term = lax.dot_general(piece, r, contract, preferred_element_type=jnp.float32)
            total_p = term if total_p is None else total_p + term
            begin += r.shape[0]
        return total_p

    residual_b_all = jnp.concatenate(residual_parts, axis=0)

    def piece(start):
        x = lax.dynamic_slice_in_dim(all_x, start, chunk, 0)
        s = lax.dynamic_slice_in_dim(all_sq, start, chunk, 0)
        r = lax.dynamic_slice_in_dim(residual_b_all, start, chunk, 0)
        c = rbf_tile(x, s, centers, centers_sq, gamma)
        return lax.dot_general(c, r, contract, preferred_element_type=jnp.float32)

    def body(i, acc):
        return acc + piece(i * chunk)

    init = jnp.zeros((centers.shape[0], residual_b_all.shape[1]), jnp.float32)
    return lax.fori_loop(0, steps, body, init)


def local(points, solution, targets, inducing, woodbury_inverse):
    gamma = 2.5 / F
    n_local = points.shape[0]
    solution_b = solution.astype(jnp.bfloat16)
    packed = jnp.concatenate([points, solution_b], axis=1)
    parts = gather_blocks(packed, split_pieces=True)
    own_sq = square_norms(points)
    kp = None
    for part in parts:
        part_x = part[:, :F]
        term = kernel_product(points, own_sq, part_x, square_norms(part_x), part[:, F:], gamma)
        kp = term if kp is None else kp + term
    residual = targets - kp - noise_level * solution
    all_x = jnp.concatenate([part[:, :F] for part in parts], axis=0)
    all_sq = square_norms(all_x)
    owner = inducing // n_local
    position = relative_order(owner) * n_local + inducing % n_local
    centers = jnp.take(all_x, position, axis=0)
    centers_sq = square_norms(centers)
    cross = rbf_tile(points, own_sq, centers, centers_sq, gamma)
    residual_b = residual.astype(jnp.bfloat16)
    res_local = jnp.sum(residual * residual, axis=0)
    tar_local = jnp.sum(targets * targets, axis=0)
    hi, lo = split_bf16(jnp.stack([res_local, tar_local]))
    extra = jnp.zeros((16, residual_b.shape[1]), jnp.bfloat16).at[0:2].set(hi).at[2:4].set(lo)
    sent = jnp.concatenate([residual_b, extra], axis=0)
    width = sent.shape[1]
    gathered_sent = gather_blocks(sent)
    got_parts = [g.reshape(-1, sent.shape[0], width) for g in gathered_sent]
    norms = sum(
        jnp.sum(g[:, n_local:n_local + 2].astype(jnp.float32) + g[:, n_local + 2:n_local + 4].astype(jnp.float32), axis=0)
        for g in got_parts
    )
    res_sq = norms[0]
    tar_sq = norms[1]
    residual_parts = [g[:, :n_local].reshape(-1, width) for g in got_parts]
    projected = projected_all(all_x, all_sq, centers, centers_sq, residual_parts, gamma)
    w_hi, w_lo = lax.optimization_barrier(split_bf16(woodbury_inverse))
    p_hi, p_lo = split_bf16(projected)
    both = jnp.dot(w_hi, jnp.concatenate([p_hi, p_lo], axis=1), preferred_element_type=jnp.float32)
    r = p_hi.shape[1]
    weights = both[:, :r] + both[:, r:] + jnp.dot(w_lo, p_hi, preferred_element_type=jnp.float32)
    correction = jnp.dot(cross, weights.astype(jnp.bfloat16), preferred_element_type=jnp.float32)
    new_solution = solution + (residual - correction) / noise_level
    relative_norm = jnp.sqrt(res_sq / (tar_sq + 1e-06))
    return (new_solution, residual, relative_norm)


def solution(mesh):
    return jax.shard_map(
        local,
        mesh=mesh,
        in_specs=(
            P(("groups", "rows", "cols"), None),
            P(("groups", "rows", "cols"), None),
            P(("groups", "rows", "cols"), None),
            P("groups"),
            P("groups", None),
        ),
        out_specs=(
            P(("groups", "rows", "cols"), None),
            P(("groups", "rows", "cols"), None),
            P("groups"),
        ),
        check_vma=False,
    )
```

```python
import jax
import jax.numpy as jnp
from jax import lax
from jax.sharding import PartitionSpec as P

F = 128


noise_level = 0.5

COLUMN_CHUNK = 3072


def square_norms(values):
    return jnp.sum(jnp.square(values.astype(jnp.float32)), axis=1)


def rbf_tile(left_x, left_sq, right_x, right_sq, gamma):
    inner = lax.dot_general(
        left_x, right_x, (((1,), (1,)), ((), ())), preferred_element_type=jnp.float32
    )
    return jnp.exp(-gamma * (left_sq[:, None] + right_sq[None, :] - 2.0 * inner)).astype(
        jnp.bfloat16
    )


def kernel_product(own_x, own_sq, all_x, all_sq, all_v, gamma):
    total = all_x.shape[0]
    chunk = min(COLUMN_CHUNK, total)
    if total % chunk != 0:
        chunk = total
    steps = total // chunk

    def piece(start):
        x = lax.dynamic_slice_in_dim(all_x, start, chunk, 0)
        s = lax.dynamic_slice_in_dim(all_sq, start, chunk, 0)
        v = lax.dynamic_slice_in_dim(all_v, start, chunk, 0)
        k = rbf_tile(own_x, own_sq, x, s, gamma)
        return jnp.dot(k, v, preferred_element_type=jnp.float32)

    if steps == 1:
        return piece(0)

    def body(i, acc):
        return acc + piece(i * chunk)

    init = jnp.zeros((own_x.shape[0], all_v.shape[1]), jnp.float32)
    return lax.fori_loop(0, steps, body, init)


def split_bf16(values):
    hi = lax.reduce_precision(values, exponent_bits=8, mantissa_bits=7)
    lo = values - hi
    return hi.astype(jnp.bfloat16), lo.astype(jnp.bfloat16)


PERMUTE_GROUP_MAX = 16


def is_power_of_two(n):
    return n & (n - 1) == 0


RING_AXES = ("rows",)


def uses_ring(axis):
    return axis in RING_AXES or not is_power_of_two(lax.axis_size(axis))


def axis_gather(value, axis):
    n = lax.axis_size(axis)
    if uses_ring(axis):
        moved = [value]
        for k in range(1, n):
            perm = [(i, (i + k) % n) for i in range(n)]
            moved.append(lax.ppermute(value, axis, perm))
        return [jnp.concatenate(moved, axis=0)]
    parts = [value]
    bit = n // 2
    while bit >= 1:
        perm = [(i, i ^ bit) for i in range(n)]
        held = parts[0] if len(parts) == 1 else jnp.concatenate(parts, axis=0)
        parts.append(lax.ppermute(held, axis, perm))
        bit //= 2
    return parts


def axis_piece(axis, owner):
    n = lax.axis_size(axis)
    me = lax.axis_index(axis)
    if uses_ring(axis):
        return (me - owner) % n
    d = me ^ owner
    steps = n.bit_length() - 1
    piece = jnp.zeros_like(d)
    for j in range(steps):
        piece = piece + (((d >> (steps - 1 - j)) & 1) << j)
    return piece


def gather_blocks(block, split_pieces=False):
    n = lax.axis_size("rows") * lax.axis_size("cols")
    if n > PERMUTE_GROUP_MAX:
        got = lax.all_gather(block, ("rows", "cols"), axis=0, tiled=False)
        order = relative_order(jnp.arange(n, dtype=jnp.int32))
        return [jnp.take(got, jnp.argsort(order), axis=0).reshape(-1, block.shape[1])]
    if not uses_ring("rows") or uses_ring("cols"):
        return axis_gather(jnp.concatenate(axis_gather(block, "rows"), axis=0), "cols")
    n_rows = lax.axis_size("rows")
    ring = [lax.ppermute(block, "rows", [(i, (i + k) % n_rows) for i in range(n_rows)]) for k in range(1, n_rows)]
    if split_pieces:
        return pipelined_xor_gather([block] + ring, "cols", split_first=True)
    return pipelined_xor_gather([block, jnp.concatenate(ring, axis=0)], "cols")


def pipelined_xor_gather(parts, axis, split_first=False):
    n = lax.axis_size(axis)
    bit = n // 2
    while bit >= 1:
        perm = [(i, i ^ bit) for i in range(n)]
        if len(parts) == 1 or (split_first and bit == n // 2):
            parts = parts + [lax.ppermute(p, axis, perm) for p in parts]
        else:
            held = lax.ppermute(jnp.concatenate(parts[:-1], axis=0), axis, perm)
            newest = lax.ppermute(parts[-1], axis, perm)
            parts = parts + [held, newest]
        bit //= 2
    return parts


def relative_order(owner):
    n_rows = lax.axis_size("rows")
    n_cols = lax.axis_size("cols")
    return axis_piece("cols", owner % n_cols) * n_rows + axis_piece("rows", owner // n_cols)


def projected_all(all_x, all_sq, centers, centers_sq, residual_parts, gamma):
    total = all_x.shape[0]
    chunk = min(COLUMN_CHUNK, total)
    if total % chunk != 0:
        chunk = total
    steps = total // chunk
    contract = (((0,), (0,)), ((), ()))

    if steps == 1:
        c = lax.optimization_barrier(rbf_tile(all_x, all_sq, centers, centers_sq, gamma))
        total_p = None
        begin = 0
        for r in residual_parts:
            piece = lax.slice_in_dim(c, begin, begin + r.shape[0], axis=0)
            term = lax.dot_general(piece, r, contract, preferred_element_type=jnp.float32)
            total_p = term if total_p is None else total_p + term
            begin += r.shape[0]
        return total_p

    residual_b_all = jnp.concatenate(residual_parts, axis=0)

    def piece(start):
        x = lax.dynamic_slice_in_dim(all_x, start, chunk, 0)
        s = lax.dynamic_slice_in_dim(all_sq, start, chunk, 0)
        r = lax.dynamic_slice_in_dim(residual_b_all, start, chunk, 0)
        c = rbf_tile(x, s, centers, centers_sq, gamma)
        return lax.dot_general(c, r, contract, preferred_element_type=jnp.float32)

    def body(i, acc):
        return acc + piece(i * chunk)

    init = jnp.zeros((centers.shape[0], residual_b_all.shape[1]), jnp.float32)
    return lax.fori_loop(0, steps, body, init)


def local(points, solution, targets, inducing, woodbury_inverse):
    gamma = 2.5 / F
    n_local = points.shape[0]
    solution_b = solution.astype(jnp.bfloat16)
    packed = jnp.concatenate([points, solution_b], axis=1)
    parts = gather_blocks(packed, split_pieces=True)
    own_sq = square_norms(points)
    kp = None
    part_sqs = []
    for part in parts:
        part_x = part[:, :F]
        part_sqs.append(square_norms(part_x))
        term = kernel_product(points, own_sq, part_x, part_sqs[-1], part[:, F:], gamma)
        kp = term if kp is None else kp + term
    residual = targets - kp - noise_level * solution
    all_x = jnp.concatenate([part[:, :F] for part in parts], axis=0)
    all_sq = jnp.concatenate(part_sqs, axis=0)
    owner = inducing // n_local
    position = relative_order(owner) * n_local + inducing % n_local
    centers = jnp.take(all_x, position, axis=0)
    centers_sq = jnp.take(all_sq, position, axis=0)
    cross = rbf_tile(points, own_sq, centers, centers_sq, gamma)
    residual_b = residual.astype(jnp.bfloat16)
    res_local = jnp.sum(residual * residual, axis=0)
    tar_local = jnp.sum(targets * targets, axis=0)
    hi, lo = split_bf16(jnp.stack([res_local, tar_local]))
    extra = jnp.zeros((16, residual_b.shape[1]), jnp.bfloat16).at[0:2].set(hi).at[2:4].set(lo)
    sent = jnp.concatenate([residual_b, extra], axis=0)
    width = sent.shape[1]
    gathered_sent = gather_blocks(sent)
    got_parts = [g.reshape(-1, sent.shape[0], width) for g in gathered_sent]
    norms = sum(
        jnp.sum(g[:, n_local:n_local + 2].astype(jnp.float32) + g[:, n_local + 2:n_local + 4].astype(jnp.float32), axis=0)
        for g in got_parts
    )
    res_sq = norms[0]
    tar_sq = norms[1]
    residual_parts = [g[:, :n_local].reshape(-1, width) for g in got_parts]
    projected = projected_all(all_x, all_sq, centers, centers_sq, residual_parts, gamma)
    w_hi, w_lo = split_bf16(woodbury_inverse)
    p_hi, p_lo = split_bf16(projected)
    both = jnp.dot(w_hi, jnp.concatenate([p_hi, p_lo], axis=1), preferred_element_type=jnp.float32)
    r = p_hi.shape[1]
    weights = both[:, :r] + both[:, r:] + jnp.dot(w_lo, p_hi, preferred_element_type=jnp.float32)
    correction = jnp.dot(cross, weights.astype(jnp.bfloat16), preferred_element_type=jnp.float32)
    new_solution = solution + (residual - correction) / noise_level
    relative_norm = jnp.sqrt(res_sq / (tar_sq + 1e-06))
    return (new_solution, residual, relative_norm)


def solution(mesh):
    return jax.shard_map(
        local,
        mesh=mesh,
        in_specs=(
            P(("groups", "rows", "cols"), None),
            P(("groups", "rows", "cols"), None),
            P(("groups", "rows", "cols"), None),
            P("groups"),
            P("groups", None),
        ),
        out_specs=(
            P(("groups", "rows", "cols"), None),
            P(("groups", "rows", "cols"), None),
            P("groups"),
        ),
        check_vma=False,
    )
```
